128 devices in a mesh: ctx: 32 (over z, y_hi, x), ch: 4 (over y_lo, core).
Axes of the slice: x: 4, y: 4 (y_hi: 2, y_lo: 2; y = y_hi * 2 + y_lo), z: 4, core: 2. Of those that a mesh axis runs over, the one named last changes fastest.
Arguments:
- q_conv: bfloat16 [7168, 4096], P('ctx', 'ch'), may hold values from -6 to 6
- k_conv: bfloat16 [7168, 4096], P('ctx', 'ch'), may hold values from -6 to 6
- v_conv: bfloat16 [7168, 4096], P('ctx', 'ch'), may hold values from -6 to 6
- conv_filter: bfloat16 [7168, 256], P('ctx', 'ch'), may hold values from -1 to 1
- q_attn: bfloat16 [7168, 4096], P('ctx', 'ch'), may hold values from -5 to 5
- k_attn: bfloat16 [7168, 4096], P('ctx', 'ch'), may hold values from -5 to 5
- v_attn: bfloat16 [7168, 4096], P('ctx', 'ch'), may hold values from -6 to 6
- w_conv_out: bfloat16 [4096, 4096], P('ch'), may hold values from -0.09375 to 0.09375
- w_attn_out: bfloat16 [4096, 4096], P('ch'), may hold values from -0.375 to 0.375
Outputs:
- layer_out: bfloat16 [7168, 4096], P(('ctx', 'ch'))
The draws below stay inside these ranges and needn't reach their ends.
All inputs are finite; a program needn't handle non-finite values.
Results may differ from the reference program's by a relative error of at most 0.018.
Values may be sent and summed in bfloat16 or wider, within the bound.
No kernel may reach another device: no remote copies, remote signals or barrier semaphores. Data moves between devices by JAX's collectives and lax.ppermute only.
A program may use at most 192 MiB of HBM per device.

```python
import math
import jax
import jax.numpy as jnp
from jax import lax

CH = 4096
GSIZE = 16
FILTER_GROUPS = 256
HEADS = 32
HD = 128
DOUT = 4096
BLK = 224
SEQUENCE_TOKENS = 7168


def attention_pair(base_key):
    width_all = HEADS * HD
    query_key = jax.random.fold_in(base_key, 11)
    keys_key = jax.random.fold_in(base_key, 12)
    queries = jnp.clip(1.4 * jax.random.normal(query_key, (SEQUENCE_TOKENS, width_all), jnp.float32), -5.0, 5.0)
    keys_drawn = jnp.clip(1.4 * jax.random.normal(keys_key, (SEQUENCE_TOKENS, width_all), jnp.float32), -5.0, 5.0)
    return (queries, keys_drawn)


def draw_q_attn(key, part):
    return attention_pair(key)[0].astype(jnp.bfloat16)


def draw_k_attn(key, part):
    return attention_pair(key)[1].astype(jnp.bfloat16)


def draw_conv_filter(key, part):
    choose_key = jax.random.fold_in(key, 21)
    slow_key = jax.random.fold_in(key, 22)
    fast_key = jax.random.fold_in(key, 23)
    noise_key = jax.random.fold_in(key, 24)
    spike_random_key = jax.random.fold_in(key, 25)
    retain_random_key = jax.random.fold_in(key, 26)
    time_positions = jnp.arange(SEQUENCE_TOKENS, dtype=jnp.float32)[:, None]
    choose = jax.random.bernoulli(choose_key, 0.5, (1, FILTER_GROUPS))
    slow_rates = jnp.exp(jax.random.uniform(slow_key, (1, FILTER_GROUPS), jnp.float32, math.log(0.1 / SEQUENCE_TOKENS), math.log(2.0 / SEQUENCE_TOKENS)))
    fast_rates = jnp.exp(jax.random.uniform(fast_key, (1, FILTER_GROUPS), jnp.float32, math.log(2.0 / SEQUENCE_TOKENS), math.log(1.0 / 30.0)))
    decay_rates = jnp.where(choose, slow_rates, fast_rates)
    noise_vals = jax.random.normal(noise_key, (SEQUENCE_TOKENS, FILTER_GROUPS), jnp.float32)
    spike_positions = jax.random.randint(spike_random_key, (3, 1, FILTER_GROUPS), 1, SEQUENCE_TOKENS)
    spike_retained = jax.random.uniform(retain_random_key, (3, 1, FILTER_GROUPS), jnp.float32, 0.5, 0.8)
    log_envelope = -decay_rates * time_positions
    for spike_total in range(3):
        elapsed_offsets = (time_positions >= spike_positions[spike_total].astype(jnp.float32)).astype(jnp.float32)
        log_envelope = log_envelope + jnp.log(spike_retained[spike_total]) * elapsed_offsets
    norm_factor = jnp.sqrt((1.0 - jnp.exp(-2.0 * decay_rates)) / (1.0 - jnp.exp(-2.0 * decay_rates * SEQUENCE_TOKENS)))
    values = jnp.clip(noise_vals, -4.0, 4.0) * jnp.exp(log_envelope) * norm_factor
    values = jnp.clip(values, -1.0, 1.0)
    values = values.at[0, 0].set(1.0)
    values = values.at[0, 1].set(-1.0)
    return values.astype(jnp.bfloat16)


def steps_of(key, dims, shards, least, top_value):
    def one(dim, blocks):
        heights = jax.random.uniform(jax.random.fold_in(jax.random.fold_in(key, 6), dim), (blocks,), jnp.float32, least / len(shards), top_value / len(shards))
        return jnp.repeat(jnp.exp(heights), dims[dim] // blocks).reshape((-1,) + (1,) * (len(dims) - dim - 1))

    loudness = one(*shards[0])
    for cut in shards[1:]:
        loudness = loudness * one(*cut)
    return loudness


def normal_values(rng, dims, scale, bound, cuts=(), kind=jnp.bfloat16):
    level = steps_of(rng, dims, cuts, -0.22, 0.18) if cuts else 1.0
    drawn = jax.random.normal(rng, dims, jnp.float32) * scale * level
    return jnp.minimum(jnp.maximum(drawn, -bound), bound).astype(kind)


def setup_inputs(seed: int = 0) -> dict:
    key_of = jax.random.split(jax.random.key(seed), 10)
    q_conv = normal_values(key_of[0], (SEQUENCE_TOKENS, CH), 1.0, 6.0, ((0, 32), (1, 4)))
    k_conv = normal_values(key_of[1], (SEQUENCE_TOKENS, CH), 1.0, 6.0, ((0, 32), (1, 4)))
    v_conv = normal_values(key_of[2], (SEQUENCE_TOKENS, CH), 1.0, 6.0, ((0, 32), (1, 4)))
    conv_filter = draw_conv_filter(jax.random.fold_in(key_of[9], 71), 0)
    q_attn = draw_q_attn(jax.random.fold_in(key_of[9], 71), 0)
    k_attn = draw_k_attn(jax.random.fold_in(key_of[9], 71), 0)
    v_attn = normal_values(key_of[6], (SEQUENCE_TOKENS, HEADS * HD), 1.0, 6.0, ((0, 32), (1, 4)))
    w_conv_out = normal_values(key_of[7], (CH, DOUT), CH ** -0.5, 0.09375, ((0, 4),))
    w_attn_out = normal_values(key_of[8], (HEADS * HD, DOUT), (2 * HD) ** -0.5, 0.375, ((0, 4),))
    return {"q_conv": q_conv, "k_conv": k_conv, "v_conv": v_conv, "conv_filter": conv_filter, "q_attn": q_attn, "k_attn": k_attn, "v_attn": v_attn, "w_conv_out": w_conv_out, "w_attn_out": w_attn_out}


def head_attention(packed):
    query_head, key_head, value_head = packed
    key_pos = jnp.arange(SEQUENCE_TOKENS, dtype=jnp.int32)
    key_wide = key_head.astype(jnp.float32)
    value_wide = value_head.astype(jnp.float32)

    def block_attention(block_number):
        first_row = block_number * BLK
        query_block = lax.dynamic_slice_in_dim(query_head, first_row, BLK, 0).astype(jnp.float32)
        scores = jnp.dot(query_block, key_wide.T, preferred_element_type=jnp.float32) * (HD ** -0.5)
        query_pos = first_row + jnp.arange(BLK, dtype=jnp.int32)
        allowed = key_pos[None, :] <= query_pos[:, None]
        row_max = jnp.max(jnp.where(allowed, scores, jnp.float32(-1e30)), axis=1, keepdims=True)
        weights = jnp.where(allowed, jnp.exp(scores - row_max), jnp.float32(0.0))
        totals = jnp.sum(weights, axis=1, keepdims=True)
        rounded = weights.astype(jnp.bfloat16).astype(jnp.float32)
        return jnp.dot(rounded, value_wide, preferred_element_type=jnp.float32) / totals

    blocks = lax.map(block_attention, jnp.arange(SEQUENCE_TOKENS // BLK, dtype=jnp.int32))
    return blocks.reshape(SEQUENCE_TOKENS, HD)


def reference(q_conv, k_conv, v_conv, conv_filter, q_attn, k_attn, v_attn, w_conv_out, w_attn_out):
    gated = (k_conv.astype(jnp.float32) * v_conv.astype(jnp.float32)).astype(jnp.bfloat16)
    length_all = 2 * SEQUENCE_TOKENS
    source_spec = jnp.fft.rfft(gated.astype(jnp.float32), n=length_all, axis=0)
    filter_spec = jnp.fft.rfft(conv_filter.astype(jnp.float32), n=length_all, axis=0)
    product = source_spec.reshape(-1, FILTER_GROUPS, GSIZE) * filter_spec[:, :, None]
    conv = jnp.fft.irfft(product.reshape(-1, CH), n=length_all, axis=0)[:SEQUENCE_TOKENS].astype(jnp.bfloat16)
    mixed = (q_conv.astype(jnp.float32) * conv.astype(jnp.float32)).astype(jnp.bfloat16)
    stacked = (q_attn.reshape(SEQUENCE_TOKENS, HEADS, HD).transpose(1, 0, 2),
               k_attn.reshape(SEQUENCE_TOKENS, HEADS, HD).transpose(1, 0, 2),
               v_attn.reshape(SEQUENCE_TOKENS, HEADS, HD).transpose(1, 0, 2))
    per_head = lax.map(head_attention, stacked)
    attended = per_head.transpose(1, 0, 2).reshape(SEQUENCE_TOKENS, HEADS * HD).astype(jnp.bfloat16)
    summed = jnp.dot(mixed, w_conv_out, preferred_element_type=jnp.float32) + jnp.dot(attended, w_attn_out, preferred_element_type=jnp.float32)
    return summed.astype(jnp.bfloat16)
```

```python
from functools import partial
import math

import jax
import jax.numpy as jnp
from jax import lax
from jax.sharding import PartitionSpec as P
from jax.experimental import pallas as pl
from jax.experimental.pallas import tpu as pltpu

HD = 128


two_pi = 2.0 * math.pi
neg_large = -1e30
highest = lax.Precision.HIGHEST


def angle_table(left_idx, right_idx, period):
    product = left_idx[:, None] * right_idx[None, :] % period
    return product.astype(jnp.float32) * (two_pi / period)


def section_coarse(values, cos_table, sin_table, twiddle):
    real_part = jnp.einsum("kn,nsc->ksc", cos_table, values, precision=highest)
    imag_part = -jnp.einsum("kn,nsc->ksc", sin_table, values, precision=highest)
    cos_twist = jnp.cos(twiddle)[:, :, None]
    sin_twist = jnp.sin(twiddle)[:, :, None]
    return (
        real_part * cos_twist + imag_part * sin_twist,
        imag_part * cos_twist - real_part * sin_twist,
    )


def section_fine(real_part, imag_part, cos_table, sin_table, direction):
    cos_real = jnp.einsum("kn,anc->akc", cos_table, real_part, precision=highest)
    cos_imag = jnp.einsum("kn,anc->akc", cos_table, imag_part, precision=highest)
    sin_real = jnp.einsum("kn,anc->akc", sin_table, real_part, precision=highest)
    sin_imag = jnp.einsum("kn,anc->akc", sin_table, imag_part, precision=highest)
    return (cos_real - direction * sin_imag, cos_imag + direction * sin_real)


def spectral_conv(gated, filters, my_index, tok_rows, count_ctx):
    chans = gated.shape[1]
    groups = filters.shape[1]
    share = chans // groups
    sub_rows = tok_rows // count_ctx
    period = 2 * count_ctx * tok_rows
    got_source, got_filter = (
        lax.all_to_all(
            gated.reshape(1, tok_rows, chans), "ctx", split_axis=1, concat_axis=0, tiled=True
        ),
        lax.all_to_all(
            filters.reshape(1, tok_rows, groups), "ctx", split_axis=1, concat_axis=0, tiled=True
        ),
    )
    coarse_idx = jnp.arange(count_ctx, dtype=jnp.int32)
    coarse_freq = jnp.arange(2 * count_ctx, dtype=jnp.int32)
    coarse_angle = angle_table(coarse_freq, coarse_idx, 2 * count_ctx)
    cos_coarse = jnp.cos(coarse_angle)
    sin_coarse = jnp.sin(coarse_angle)
    fine_global = my_index * sub_rows + jnp.arange(sub_rows, dtype=jnp.int32)
    twist_in = angle_table(coarse_freq, fine_global, period)
    source_re, source_im = section_coarse(
        got_source.astype(jnp.float32), cos_coarse, sin_coarse, twist_in
    )
    filter_re, filter_im = section_coarse(
        got_filter.astype(jnp.float32), cos_coarse, sin_coarse, twist_in
    )
    source_re, source_im, filter_re, filter_im = (
        lax.all_to_all(
            source_re.astype(jnp.bfloat16), "ctx", split_axis=0, concat_axis=1, tiled=True
        ).astype(source_re.dtype),
        lax.all_to_all(
            source_im.astype(jnp.bfloat16), "ctx", split_axis=0, concat_axis=1, tiled=True
        ).astype(source_im.dtype),
        lax.all_to_all(
            filter_re.astype(jnp.bfloat16), "ctx", split_axis=0, concat_axis=1, tiled=True
        ).astype(filter_re.dtype),
        lax.all_to_all(
            filter_im.astype(jnp.bfloat16), "ctx", split_axis=0, concat_axis=1, tiled=True
        ).astype(filter_im.dtype),
    )
    fine_idx = jnp.arange(tok_rows, dtype=jnp.int32)
    fine_angle = angle_table(fine_idx, fine_idx, tok_rows)
    cos_fine = jnp.cos(fine_angle)
    sin_fine = jnp.sin(fine_angle)
    source_re, source_im = section_fine(source_re, source_im, cos_fine, sin_fine, -1.0)
    filter_re, filter_im = section_fine(filter_re, filter_im, cos_fine, sin_fine, -1.0)
    split_re = source_re.reshape(2, tok_rows, groups, share)
    split_im = source_im.reshape(2, tok_rows, groups, share)
    prod_re = split_re * filter_re[..., None] - split_im * filter_im[..., None]
    prod_im = split_re * filter_im[..., None] + split_im * filter_re[..., None]
    back_re, back_im = section_fine(
        prod_re.reshape(2, tok_rows, chans),
        prod_im.reshape(2, tok_rows, chans),
        cos_fine,
        sin_fine,
        1.0,
    )
    pair_freq = my_index * 2 + jnp.arange(2, dtype=jnp.int32)
    twist_out = angle_table(pair_freq, fine_idx, period)
    cos_out = jnp.cos(twist_out)[:, :, None]
    sin_out = jnp.sin(twist_out)[:, :, None]
    turned_re = back_re * cos_out - back_im * sin_out
    turned_im = back_re * sin_out + back_im * cos_out
    turned_re, turned_im = (
        lax.all_to_all(
            turned_re.astype(jnp.bfloat16), "ctx", split_axis=1, concat_axis=0, tiled=True
        ).astype(turned_re.dtype),
        lax.all_to_all(
            turned_im.astype(jnp.bfloat16), "ctx", split_axis=1, concat_axis=0, tiled=True
        ).astype(turned_im.dtype),
    )
    result = jnp.einsum("nk,ksc->nsc", cos_coarse.T, turned_re, precision=highest)
    result = result - jnp.einsum("nk,ksc->nsc", sin_coarse.T, turned_im, precision=highest)
    rounded = (result / period).astype(jnp.bfloat16)
    returned = lax.all_to_all(rounded, "ctx", split_axis=0, concat_axis=1, tiled=True)
    return returned.reshape(tok_rows, chans)


KEY_BLOCK = 1024


def flash_kernel(info_ref, q_ref, k_ref, v_ref, o_ref, m_sc, l_sc, acc_sc, *, heads, tok_rows, key_block, scale):
    j = pl.program_id(0)
    q_first = info_ref[0] * tok_rows
    last_block = info_ref[1] - 1
    key_first = j * key_block

    @pl.when(j == 0)
    def _():
        m_sc[...] = jnp.full_like(m_sc, neg_large)
        l_sc[...] = jnp.zeros_like(l_sc)
        acc_sc[...] = jnp.zeros_like(acc_sc)

    def step(masked):
        if masked:
            query_pos = q_first + lax.broadcasted_iota(jnp.int32, (tok_rows, key_block), 0)
            key_pos = key_first + lax.broadcasted_iota(jnp.int32, (tok_rows, key_block), 1)
            allowed = key_pos <= query_pos
        for h in range(heads):
            cols = slice(h * HD, (h + 1) * HD)
            scores = lax.dot_general(
                q_ref[:, cols], k_ref[:, cols], (((1,), (1,)), ((), ())),
                preferred_element_type=jnp.float32,
            ) * scale
            if masked:
                scores = jnp.where(allowed, scores, neg_large)
            m_prev = m_sc[h]
            m_new = jnp.maximum(m_prev, jnp.max(scores, axis=1, keepdims=True))
            weights = jnp.exp(scores - m_new)
            if masked:
                weights = jnp.where(allowed, weights, 0.0)
            factor = jnp.exp(m_prev - m_new)
            l_sc[h] = l_sc[h] * factor + jnp.sum(weights, axis=1, keepdims=True)
            acc_sc[:, cols] = acc_sc[:, cols] * factor + jnp.dot(
                weights.astype(jnp.bfloat16), v_ref[:, cols], preferred_element_type=jnp.float32
            )
            m_sc[h] = m_new

    full = key_first + key_block <= q_first

    @pl.when(jnp.logical_and(j <= last_block, full))
    def _():
        step(False)

    @pl.when(jnp.logical_and(j <= last_block, jnp.logical_not(full)))
    def _():
        step(True)

    @pl.when(j == last_block)
    def _():
        for h in range(heads):
            cols = slice(h * HD, (h + 1) * HD)
            o_ref[:, cols] = (acc_sc[:, cols] / l_sc[h]).astype(o_ref.dtype)


def attention(q_attn, k_attn, v_attn, my_index, tok_rows):
    width = q_attn.shape[1]
    heads_local = width // HD
    key_piece = lax.all_gather(k_attn, "ctx", axis=0, tiled=True)
    value_piece = lax.all_gather(v_attn, "ctx", axis=0, tiled=True)
    return attention_core(q_attn, key_piece, value_piece, my_index, tok_rows)


def attention_core(q_attn, key_piece, value_piece, my_index, tok_rows):
    width = q_attn.shape[1]
    heads_local = width // HD
    total_rows = key_piece.shape[0]
    key_block = KEY_BLOCK if total_rows % KEY_BLOCK == 0 else tok_rows
    count_blocks = total_rows // key_block
    needed = ((my_index + 1) * tok_rows + key_block - 1) // key_block
    info = jnp.stack([my_index, needed]).astype(jnp.int32)
    kernel = partial(
        flash_kernel, heads=heads_local, tok_rows=tok_rows, key_block=key_block, scale=HD ** (-0.5)
    )
    kv_spec = pl.BlockSpec((key_block, width), lambda j, info: (jnp.minimum(j, info[1] - 1), 0))
    return pl.pallas_call(
        kernel,
        out_shape=jax.ShapeDtypeStruct((tok_rows, width), jnp.bfloat16),
        grid_spec=pltpu.PrefetchScalarGridSpec(
            num_scalar_prefetch=1,
            grid=(count_blocks,),
            in_specs=[
                pl.BlockSpec((tok_rows, width), lambda j, info: (0, 0)),
                kv_spec,
                kv_spec,
            ],
            out_specs=pl.BlockSpec((tok_rows, width), lambda j, info: (0, 0)),
            scratch_shapes=[
                pltpu.VMEM((heads_local, tok_rows, 1), jnp.float32),
                pltpu.VMEM((heads_local, tok_rows, 1), jnp.float32),
                pltpu.VMEM((tok_rows, width), jnp.float32),
            ],
        ),
        compiler_params=pltpu.CompilerParams(
            dimension_semantics=("arbitrary",), vmem_limit_bytes=48 * 1024 * 1024
        ),
        cost_estimate=pl.CostEstimate(
            flops=4 * tok_rows * total_rows * width,
            transcendentals=heads_local * tok_rows * total_rows,
            bytes_accessed=2 * total_rows * width * 2 + 2 * tok_rows * width * 2,
        ),
    )(info, q_attn, key_piece, value_piece)


def local(q_conv, k_conv, v_conv, conv_filter, q_attn, k_attn, v_attn, w_conv_out, w_attn_out):
    count_ctx = lax.axis_size("ctx")
    my_index = lax.axis_index("ctx")
    tok_rows = q_conv.shape[0]
    gated = (k_conv.astype(jnp.float32) * v_conv.astype(jnp.float32)).astype(jnp.bfloat16)
    conv = spectral_conv(gated, conv_filter, my_index, tok_rows, count_ctx)
    mixed = (q_conv.astype(jnp.float32) * conv.astype(jnp.float32)).astype(jnp.bfloat16)
    attended = attention(q_attn, k_attn, v_attn, my_index, tok_rows)
    return lax.psum_scatter(
        (
            jnp.dot(mixed, w_conv_out, preferred_element_type=jnp.float32)
            + jnp.dot(attended, w_attn_out, preferred_element_type=jnp.float32)
        ).astype(jnp.bfloat16),
        "ch",
        scatter_dimension=0,
        tiled=True,
    )


def solution(mesh):
    return jax.shard_map(
        local,
        mesh=mesh,
        in_specs=(
            P("ctx", "ch"),
            P("ctx", "ch"),
            P("ctx", "ch"),
            P("ctx", "ch"),
            P("ctx", "ch"),
            P("ctx", "ch"),
            P("ctx", "ch"),
            P("ch", None),
            P("ch", None),
        ),
        out_specs=P(("ctx", "ch"), None),
        check_vma=False,
    )
```

```python
from functools import partial
import math

import jax
import jax.numpy as jnp
from jax import lax
from jax.sharding import PartitionSpec as P
from jax.experimental import pallas as pl
from jax.experimental.pallas import tpu as pltpu

HD = 128


two_pi = 2.0 * math.pi
neg_large = -1e30
highest = lax.Precision.HIGHEST


def angle_table(left_idx, right_idx, period):
    product = left_idx[:, None] * right_idx[None, :] % period
    return product.astype(jnp.float32) * (two_pi / period)


def section_coarse(values, cos_table, sin_table, twiddle):
    real_part = jnp.einsum("kn,nsc->ksc", cos_table, values, precision=highest)
    imag_part = -jnp.einsum("kn,nsc->ksc", sin_table, values, precision=highest)
    cos_twist = jnp.cos(twiddle)[:, :, None]
    sin_twist = jnp.sin(twiddle)[:, :, None]
    return (
        real_part * cos_twist + imag_part * sin_twist,
        imag_part * cos_twist - real_part * sin_twist,
    )


def section_fine(real_part, imag_part, cos_table, sin_table, direction):
    cos_real = jnp.einsum("kn,anc->akc", cos_table, real_part, precision=highest)
    cos_imag = jnp.einsum("kn,anc->akc", cos_table, imag_part, precision=highest)
    sin_real = jnp.einsum("kn,anc->akc", sin_table, real_part, precision=highest)
    sin_imag = jnp.einsum("kn,anc->akc", sin_table, imag_part, precision=highest)
    return (cos_real - direction * sin_imag, cos_imag + direction * sin_real)


def spectral_conv(gated, filters, my_index, tok_rows, count_ctx):
    chans = gated.shape[1]
    groups = filters.shape[1]
    share = chans // groups
    sub_rows = tok_rows // count_ctx
    period = 2 * count_ctx * tok_rows
    got_source, got_filter = (
        lax.all_to_all(
            gated.reshape(1, tok_rows, chans), CTX, split_axis=1, concat_axis=0, tiled=True
        ),
        lax.all_to_all(
            filters.reshape(1, tok_rows, groups), CTX, split_axis=1, concat_axis=0, tiled=True
        ),
    )
    coarse_idx = jnp.arange(count_ctx, dtype=jnp.int32)
    coarse_freq = jnp.arange(2 * count_ctx, dtype=jnp.int32)
    coarse_angle = angle_table(coarse_freq, coarse_idx, 2 * count_ctx)
    cos_coarse = jnp.cos(coarse_angle)
    sin_coarse = jnp.sin(coarse_angle)
    fine_global = my_index * sub_rows + jnp.arange(sub_rows, dtype=jnp.int32)
    twist_in = angle_table(coarse_freq, fine_global, period)
    source_re, source_im = section_coarse(
        got_source.astype(jnp.float32), cos_coarse, sin_coarse, twist_in
    )
    filter_re, filter_im = section_coarse(
        got_filter.astype(jnp.float32), cos_coarse, sin_coarse, twist_in
    )
    source_re, source_im, filter_re, filter_im = (
        lax.all_to_all(
            source_re.astype(jnp.bfloat16), CTX, split_axis=0, concat_axis=1, tiled=True
        ).astype(source_re.dtype),
        lax.all_to_all(
            source_im.astype(jnp.bfloat16), CTX, split_axis=0, concat_axis=1, tiled=True
        ).astype(source_im.dtype),
        lax.all_to_all(
            filter_re.astype(jnp.bfloat16), CTX, split_axis=0, concat_axis=1, tiled=True
        ).astype(filter_re.dtype),
        lax.all_to_all(
            filter_im.astype(jnp.bfloat16), CTX, split_axis=0, concat_axis=1, tiled=True
        ).astype(filter_im.dtype),
    )
    fine_idx = jnp.arange(tok_rows, dtype=jnp.int32)
    fine_angle = angle_table(fine_idx, fine_idx, tok_rows)
    cos_fine = jnp.cos(fine_angle)
    sin_fine = jnp.sin(fine_angle)
    source_re, source_im = section_fine(source_re, source_im, cos_fine, sin_fine, -1.0)
    filter_re, filter_im = section_fine(filter_re, filter_im, cos_fine, sin_fine, -1.0)
    split_re = source_re.reshape(2, tok_rows, groups, share)
    split_im = source_im.reshape(2, tok_rows, groups, share)
    prod_re = split_re * filter_re[..., None] - split_im * filter_im[..., None]
    prod_im = split_re * filter_im[..., None] + split_im * filter_re[..., None]
    back_re, back_im = section_fine(
        prod_re.reshape(2, tok_rows, chans),
        prod_im.reshape(2, tok_rows, chans),
        cos_fine,
        sin_fine,
        1.0,
    )
    pair_freq = my_index * 2 + jnp.arange(2, dtype=jnp.int32)
    twist_out = angle_table(pair_freq, fine_idx, period)
    cos_out = jnp.cos(twist_out)[:, :, None]
    sin_out = jnp.sin(twist_out)[:, :, None]
    turned_re = back_re * cos_out - back_im * sin_out
    turned_im = back_re * sin_out + back_im * cos_out
    turned_re, turned_im = (
        lax.all_to_all(
            turned_re.astype(jnp.bfloat16), CTX, split_axis=1, concat_axis=0, tiled=True
        ).astype(turned_re.dtype),
        lax.all_to_all(
            turned_im.astype(jnp.bfloat16), CTX, split_axis=1, concat_axis=0, tiled=True
        ).astype(turned_im.dtype),
    )
    result = jnp.einsum("nk,ksc->nsc", cos_coarse.T, turned_re, precision=highest)
    result = result - jnp.einsum("nk,ksc->nsc", sin_coarse.T, turned_im, precision=highest)
    rounded = (result / period).astype(jnp.bfloat16)
    returned = lax.all_to_all(rounded, CTX, split_axis=0, concat_axis=1, tiled=True)
    return returned.reshape(tok_rows, chans)


CTX = ("z", "yh", "x")


def flash_kernel(info_ref, q_ref, k_ref, v_ref, o_ref, m_sc, l_sc, acc_sc, *, heads, tok_rows, x_size, yh_size, scale):
    j = pl.program_id(0)
    my_ctx = info_ref[0]
    last_block = info_ref[1] - 1
    z = j // x_size
    x = j % x_size

    @pl.when(j == 0)
    def _():
        m_sc[...] = jnp.full_like(m_sc, neg_large)
        l_sc[...] = jnp.zeros_like(l_sc)
        acc_sc[...] = jnp.zeros_like(acc_sc)

    def step(half, masked):
        if masked:
            query_pos = lax.broadcasted_iota(jnp.int32, (tok_rows, tok_rows), 0)
            key_pos = lax.broadcasted_iota(jnp.int32, (tok_rows, tok_rows), 1)
            allowed = key_pos <= query_pos
        for h in range(heads):
            cols = slice(h * HD, (h + 1) * HD)
            scores = lax.dot_general(
                q_ref[:, cols], k_ref[half, :, cols], (((1,), (1,)), ((), ())),
                preferred_element_type=jnp.float32,
            ) * scale
            if masked:
                scores = jnp.where(allowed, scores, neg_large)
            m_prev = m_sc[h]
            m_new = jnp.maximum(m_prev, jnp.max(scores, axis=1, keepdims=True))
            weights = jnp.exp(scores - m_new)
            if masked:
                weights = jnp.where(allowed, weights, 0.0)
            factor = jnp.exp(m_prev - m_new)
            l_sc[h] = l_sc[h] * factor + jnp.sum(weights, axis=1, keepdims=True)
            acc_sc[:, cols] = acc_sc[:, cols] * factor + jnp.dot(
                weights.astype(jnp.bfloat16), v_ref[half, :, cols], preferred_element_type=jnp.float32
            )
            m_sc[h] = m_new

    for half in range(yh_size):
        block_ctx = (z * yh_size + half) * x_size + x
        active = j <= last_block

        @pl.when(jnp.logical_and(active, block_ctx < my_ctx))
        def _():
            step(half, False)

        @pl.when(jnp.logical_and(active, block_ctx == my_ctx))
        def _():
            step(half, True)

    @pl.when(j == last_block)
    def _():
        for h in range(heads):
            cols = slice(h * HD, (h + 1) * HD)
            o_ref[:, cols] = (acc_sc[:, cols] / l_sc[h]).astype(o_ref.dtype)


def attention(q_attn, k_attn, v_attn, tok_rows):
    width = q_attn.shape[1]
    heads_local = width // HD
    z_size, yh_size, x_size = (lax.axis_size(name) for name in CTX)
    z_me, yh_me, x_me = (lax.axis_index(name) for name in CTX)
    my_ctx = (z_me * yh_size + yh_me) * x_size + x_me
    both = jnp.stack([k_attn, v_attn])
    across = lax.all_gather(both, "yh", axis=0)
    gathered = lax.all_gather(across, ("z", "x"), axis=0)
    count_blocks = z_size * x_size
    needed = z_me * x_size + jnp.where(yh_me == 0, x_me + 1, x_size)
    info = jnp.stack([my_ctx, needed]).astype(jnp.int32)
    kernel = partial(
        flash_kernel, heads=heads_local, tok_rows=tok_rows, x_size=x_size, yh_size=yh_size,
        scale=HD ** (-0.5),
    )
    total_rows = count_blocks * yh_size * tok_rows
    return pl.pallas_call(
        kernel,
        out_shape=jax.ShapeDtypeStruct((tok_rows, width), jnp.bfloat16),
        grid_spec=pltpu.PrefetchScalarGridSpec(
            num_scalar_prefetch=1,
            grid=(count_blocks,),
            in_specs=[
                pl.BlockSpec((tok_rows, width), lambda j, info: (0, 0)),
                pl.BlockSpec(
                    (None, yh_size, None, tok_rows, width),
                    lambda j, info: (jnp.minimum(j, info[1] - 1), 0, 0, 0, 0),
                ),
                pl.BlockSpec(
                    (None, yh_size, None, tok_rows, width),
                    lambda j, info: (jnp.minimum(j, info[1] - 1), 0, 1, 0, 0),
                ),
            ],
            out_specs=pl.BlockSpec((tok_rows, width), lambda j, info: (0, 0)),
            scratch_shapes=[
                pltpu.VMEM((heads_local, tok_rows, 1), jnp.float32),
                pltpu.VMEM((heads_local, tok_rows, 1), jnp.float32),
                pltpu.VMEM((tok_rows, width), jnp.float32),
            ],
        ),
        compiler_params=pltpu.CompilerParams(
            dimension_semantics=("arbitrary",), vmem_limit_bytes=48 * 1024 * 1024
        ),
        cost_estimate=pl.CostEstimate(
            flops=4 * tok_rows * total_rows * width,
            transcendentals=heads_local * tok_rows * total_rows,
            bytes_accessed=2 * total_rows * width * 2 + 2 * tok_rows * width * 2,
        ),
    )(info, q_attn, gathered, gathered)


def local(q_conv, k_conv, v_conv, conv_filter, q_attn, k_attn, v_attn, w_conv_out, w_attn_out):
    z_size, yh_size, x_size = (lax.axis_size(name) for name in CTX)
    z_me, yh_me, x_me = (lax.axis_index(name) for name in CTX)
    count_ctx = z_size * yh_size * x_size
    my_index = (z_me * yh_size + yh_me) * x_size + x_me
    tok_rows = q_conv.shape[0]
    gated = (k_conv.astype(jnp.float32) * v_conv.astype(jnp.float32)).astype(jnp.bfloat16)
    conv = spectral_conv(gated, conv_filter, my_index, tok_rows, count_ctx)
    mixed = (q_conv.astype(jnp.float32) * conv.astype(jnp.float32)).astype(jnp.bfloat16)
    attended = attention(q_attn, k_attn, v_attn, tok_rows)
    return lax.psum_scatter(
        (
            jnp.dot(mixed, w_conv_out, preferred_element_type=jnp.float32)
            + jnp.dot(attended, w_attn_out, preferred_element_type=jnp.float32)
        ).astype(jnp.bfloat16),
        "ch",
        scatter_dimension=0,
        tiled=True,
    )


def solution(mesh):
    ctx_size, ch_size = mesh.devices.shape
    x_size = 4
    yh_size = 2
    z_size = ctx_size // (x_size * yh_size)
    split_mesh = jax.sharding.Mesh(
        mesh.devices.reshape(z_size, yh_size, x_size, ch_size), ("z", "yh", "x", "ch")
    )
    tokens = P(CTX, "ch")
    return jax.shard_map(
        local,
        mesh=split_mesh,
        in_specs=(tokens,) * 7 + (P("ch", None), P("ch", None)),
        out_specs=P(CTX + ("ch",), None),
        check_vma=False,
    )
```

```python
from functools import partial
import math

import jax
import jax.numpy as jnp
from jax import lax
from jax.sharding import PartitionSpec as P
from jax.experimental import pallas as pl
from jax.experimental.pallas import tpu as pltpu

HD = 128


two_pi = 2.0 * math.pi
neg_large = -1e30
highest = lax.Precision.HIGHEST


def angle_table(left_idx, right_idx, period):
    product = left_idx[:, None] * right_idx[None, :] % period
    return product.astype(jnp.float32) * (two_pi / period)


def section_coarse(values, cos_table, sin_table, twiddle):
    real_part = jnp.einsum("kn,nsc->ksc", cos_table, values, precision=highest)
    imag_part = -jnp.einsum("kn,nsc->ksc", sin_table, values, precision=highest)
    cos_twist = jnp.cos(twiddle)[:, :, None]
    sin_twist = jnp.sin(twiddle)[:, :, None]
    return (
        real_part * cos_twist + imag_part * sin_twist,
        imag_part * cos_twist - real_part * sin_twist,
    )


def section_fine(real_part, imag_part, cos_table, sin_table, direction):
    cos_real = jnp.einsum("kn,anc->akc", cos_table, real_part, precision=highest)
    cos_imag = jnp.einsum("kn,anc->akc", cos_table, imag_part, precision=highest)
    sin_real = jnp.einsum("kn,anc->akc", sin_table, real_part, precision=highest)
    sin_imag = jnp.einsum("kn,anc->akc", sin_table, imag_part, precision=highest)
    return (cos_real - direction * sin_imag, cos_imag + direction * sin_real)


def spectral_conv(gated, filters, my_index, tok_rows, count_ctx):
    chans = gated.shape[1]
    groups = filters.shape[1]
    share = chans // groups
    sub_rows = tok_rows // count_ctx
    period = 2 * count_ctx * tok_rows
    got_source, got_filter = (
        lax.all_to_all(
            gated.reshape(1, tok_rows, chans), "ctx", split_axis=1, concat_axis=0, tiled=True
        ),
        lax.all_to_all(
            filters.reshape(1, tok_rows, groups), "ctx", split_axis=1, concat_axis=0, tiled=True
        ),
    )
    coarse_idx = jnp.arange(count_ctx, dtype=jnp.int32)
    coarse_freq = jnp.arange(2 * count_ctx, dtype=jnp.int32)
    coarse_angle = angle_table(coarse_freq, coarse_idx, 2 * count_ctx)
    cos_coarse = jnp.cos(coarse_angle)
    sin_coarse = jnp.sin(coarse_angle)
    fine_global = my_index * sub_rows + jnp.arange(sub_rows, dtype=jnp.int32)
    twist_in = angle_table(coarse_freq, fine_global, period)
    source_re, source_im = section_coarse(
        got_source.astype(jnp.float32), cos_coarse, sin_coarse, twist_in
    )
    filter_re, filter_im = section_coarse(
        got_filter.astype(jnp.float32), cos_coarse, sin_coarse, twist_in
    )
    source_re, source_im, filter_re, filter_im = (
        lax.all_to_all(
            source_re.astype(jnp.bfloat16), "ctx", split_axis=0, concat_axis=1, tiled=True
        ).astype(source_re.dtype),
        lax.all_to_all(
            source_im.astype(jnp.bfloat16), "ctx", split_axis=0, concat_axis=1, tiled=True
        ).astype(source_im.dtype),
        lax.all_to_all(
            filter_re.astype(jnp.bfloat16), "ctx", split_axis=0, concat_axis=1, tiled=True
        ).astype(filter_re.dtype),
        lax.all_to_all(
            filter_im.astype(jnp.bfloat16), "ctx", split_axis=0, concat_axis=1, tiled=True
        ).astype(filter_im.dtype),
    )
    fine_idx = jnp.arange(tok_rows, dtype=jnp.int32)
    fine_angle = angle_table(fine_idx, fine_idx, tok_rows)
    cos_fine = jnp.cos(fine_angle)
    sin_fine = jnp.sin(fine_angle)
    source_re, source_im = section_fine(source_re, source_im, cos_fine, sin_fine, -1.0)
    filter_re, filter_im = section_fine(filter_re, filter_im, cos_fine, sin_fine, -1.0)
    split_re = source_re.reshape(2, tok_rows, groups, share)
    split_im = source_im.reshape(2, tok_rows, groups, share)
    prod_re = split_re * filter_re[..., None] - split_im * filter_im[..., None]
    prod_im = split_re * filter_im[..., None] + split_im * filter_re[..., None]
    back_re, back_im = section_fine(
        prod_re.reshape(2, tok_rows, chans),
        prod_im.reshape(2, tok_rows, chans),
        cos_fine,
        sin_fine,
        1.0,
    )
    pair_freq = my_index * 2 + jnp.arange(2, dtype=jnp.int32)
    twist_out = angle_table(pair_freq, fine_idx, period)
    cos_out = jnp.cos(twist_out)[:, :, None]
    sin_out = jnp.sin(twist_out)[:, :, None]
    turned_re = back_re * cos_out - back_im * sin_out
    turned_im = back_re * sin_out + back_im * cos_out
    turned_re, turned_im = (
        lax.all_to_all(
            turned_re.astype(jnp.bfloat16), "ctx", split_axis=1, concat_axis=0, tiled=True
        ).astype(turned_re.dtype),
        lax.all_to_all(
            turned_im.astype(jnp.bfloat16), "ctx", split_axis=1, concat_axis=0, tiled=True
        ).astype(turned_im.dtype),
    )
    result = jnp.einsum("nk,ksc->nsc", cos_coarse.T, turned_re, precision=highest)
    result = result - jnp.einsum("nk,ksc->nsc", sin_coarse.T, turned_im, precision=highest)
    rounded = (result / period).astype(jnp.bfloat16)
    returned = lax.all_to_all(rounded, "ctx", split_axis=0, concat_axis=1, tiled=True)
    return returned.reshape(tok_rows, chans)


KEY_BLOCK = 1024


def flash_kernel(info_ref, q_ref, k_ref, v_ref, o_ref, m_sc, l_sc, acc_sc, *, heads, tok_rows, key_block, scale):
    j = pl.program_id(0)
    q_first = info_ref[0] * tok_rows
    last_block = info_ref[1] - 1
    key_first = j * key_block

    @pl.when(j == 0)
    def _():
        m_sc[...] = jnp.full_like(m_sc, neg_large)
        l_sc[...] = jnp.zeros_like(l_sc)
        acc_sc[...] = jnp.zeros_like(acc_sc)

    def step(masked):
        if masked:
            query_pos = q_first + lax.broadcasted_iota(jnp.int32, (tok_rows, key_block), 0)
            key_pos = key_first + lax.broadcasted_iota(jnp.int32, (tok_rows, key_block), 1)
            allowed = key_pos <= query_pos
        for h in range(heads):
            cols = slice(h * HD, (h + 1) * HD)
            scores = lax.dot_general(
                q_ref[:, cols], k_ref[:, cols], (((1,), (1,)), ((), ())),
                preferred_element_type=jnp.float32,
            ) * scale
            if masked:
                scores = jnp.where(allowed, scores, neg_large)
            m_prev = m_sc[h]
            m_new = jnp.maximum(m_prev, jnp.max(scores, axis=1, keepdims=True))
            weights = jnp.exp(scores - m_new)
            if masked:
                weights = jnp.where(allowed, weights, 0.0)
            factor = jnp.exp(m_prev - m_new)
            l_sc[h] = l_sc[h] * factor + jnp.sum(weights, axis=1, keepdims=True)
            acc_sc[:, cols] = acc_sc[:, cols] * factor + jnp.dot(
                weights.astype(jnp.bfloat16), v_ref[:, cols], preferred_element_type=jnp.float32
            )
            m_sc[h] = m_new

    full = key_first + key_block <= q_first

    @pl.when(jnp.logical_and(j <= last_block, full))
    def _():
        step(False)

    @pl.when(jnp.logical_and(j <= last_block, jnp.logical_not(full)))
    def _():
        step(True)

    @pl.when(j == last_block)
    def _():
        for h in range(heads):
            cols = slice(h * HD, (h + 1) * HD)
            o_ref[:, cols] = (acc_sc[:, cols] / l_sc[h]).astype(o_ref.dtype)


def attention(q_attn, k_attn, v_attn, my_index, tok_rows):
    width = q_attn.shape[1]
    heads_local = width // HD
    key_piece = lax.all_gather(k_attn, "ctx", axis=0, tiled=True)
    count_ctx = lax.axis_size("ctx")
    copies = jnp.broadcast_to(v_attn[None], (count_ctx,) + v_attn.shape)
    value_piece = lax.all_to_all(copies, "ctx", split_axis=0, concat_axis=0, tiled=True).reshape(
        count_ctx * v_attn.shape[0], v_attn.shape[1]
    )
    return attention_core(q_attn, key_piece, value_piece, my_index, tok_rows)


def attention_core(q_attn, key_piece, value_piece, my_index, tok_rows):
    width = q_attn.shape[1]
    heads_local = width // HD
    total_rows = key_piece.shape[0]
    key_block = KEY_BLOCK if total_rows % KEY_BLOCK == 0 else tok_rows
    count_blocks = total_rows // key_block
    needed = ((my_index + 1) * tok_rows + key_block - 1) // key_block
    info = jnp.stack([my_index, needed]).astype(jnp.int32)
    kernel = partial(
        flash_kernel, heads=heads_local, tok_rows=tok_rows, key_block=key_block, scale=HD ** (-0.5)
    )
    kv_spec = pl.BlockSpec((key_block, width), lambda j, info: (jnp.minimum(j, info[1] - 1), 0))
    return pl.pallas_call(
        kernel,
        out_shape=jax.ShapeDtypeStruct((tok_rows, width), jnp.bfloat16),
        grid_spec=pltpu.PrefetchScalarGridSpec(
            num_scalar_prefetch=1,
            grid=(count_blocks,),
            in_specs=[
                pl.BlockSpec((tok_rows, width), lambda j, info: (0, 0)),
                kv_spec,
                kv_spec,
            ],
            out_specs=pl.BlockSpec((tok_rows, width), lambda j, info: (0, 0)),
            scratch_shapes=[
                pltpu.VMEM((heads_local, tok_rows, 1), jnp.float32),
                pltpu.VMEM((heads_local, tok_rows, 1), jnp.float32),
                pltpu.VMEM((tok_rows, width), jnp.float32),
            ],
        ),
        compiler_params=pltpu.CompilerParams(
            dimension_semantics=("arbitrary",), vmem_limit_bytes=48 * 1024 * 1024
        ),
        cost_estimate=pl.CostEstimate(
            flops=4 * tok_rows * total_rows * width,
            transcendentals=heads_local * tok_rows * total_rows,
            bytes_accessed=2 * total_rows * width * 2 + 2 * tok_rows * width * 2,
        ),
    )(info, q_attn, key_piece, value_piece)


def local(q_conv, k_conv, v_conv, conv_filter, q_attn, k_attn, v_attn, w_conv_out, w_attn_out):
    count_ctx = lax.axis_size("ctx")
    my_index = lax.axis_index("ctx")
    tok_rows = q_conv.shape[0]
    gated = (k_conv.astype(jnp.float32) * v_conv.astype(jnp.float32)).astype(jnp.bfloat16)
    conv = spectral_conv(gated, conv_filter, my_index, tok_rows, count_ctx)
    mixed = (q_conv.astype(jnp.float32) * conv.astype(jnp.float32)).astype(jnp.bfloat16)
    attended = attention(q_attn, k_attn, v_attn, my_index, tok_rows)
    return lax.psum_scatter(
        (
            jnp.dot(mixed, w_conv_out, preferred_element_type=jnp.float32)
            + jnp.dot(attended, w_attn_out, preferred_element_type=jnp.float32)
        ).astype(jnp.bfloat16),
        "ch",
        scatter_dimension=0,
        tiled=True,
    )


def solution(mesh):
    return jax.shard_map(
        local,
        mesh=mesh,
        in_specs=(
            P("ctx", "ch"),
            P("ctx", "ch"),
            P("ctx", "ch"),
            P("ctx", "ch"),
            P("ctx", "ch"),
            P("ctx", "ch"),
            P("ctx", "ch"),
            P("ch", None),
            P("ch", None),
        ),
        out_specs=P(("ctx", "ch"), None),
        check_vma=False,
    )
```

```python
from functools import partial
import math

import jax
import jax.numpy as jnp
from jax import lax
from jax.sharding import PartitionSpec as P
from jax.experimental import pallas as pl
from jax.experimental.pallas import tpu as pltpu

HD = 128


two_pi = 2.0 * math.pi
neg_large = -1e30
highest = lax.Precision.HIGHEST


def angle_table(left_idx, right_idx, period):
    product = left_idx[:, None] * right_idx[None, :] % period
    return product.astype(jnp.float32) * (two_pi / period)


def section_coarse(values, cos_table, sin_table, twiddle):
    real_part = jnp.einsum("kn,nsc->ksc", cos_table, values, precision=highest)
    imag_part = -jnp.einsum("kn,nsc->ksc", sin_table, values, precision=highest)
    cos_twist = jnp.cos(twiddle)[:, :, None]
    sin_twist = jnp.sin(twiddle)[:, :, None]
    return (
        real_part * cos_twist + imag_part * sin_twist,
        imag_part * cos_twist - real_part * sin_twist,
    )


def section_fine(real_part, imag_part, cos_table, sin_table, direction):
    cos_real = jnp.einsum("kn,anc->akc", cos_table, real_part, precision=highest)
    cos_imag = jnp.einsum("kn,anc->akc", cos_table, imag_part, precision=highest)
    sin_real = jnp.einsum("kn,anc->akc", sin_table, real_part, precision=highest)
    sin_imag = jnp.einsum("kn,anc->akc", sin_table, imag_part, precision=highest)
    return (cos_real - direction * sin_imag, cos_imag + direction * sin_real)


def spectral_conv(gated, filters, my_index, tok_rows, count_ctx):
    chans = gated.shape[1]
    groups = filters.shape[1]
    share = chans // groups
    sub_rows = tok_rows // count_ctx
    period = 2 * count_ctx * tok_rows
    got_source, got_filter = (
        lax.all_to_all(
            gated.reshape(1, tok_rows, chans), CTX, split_axis=1, concat_axis=0, tiled=True
        ),
        lax.all_to_all(
            filters.reshape(1, tok_rows, groups), CTX, split_axis=1, concat_axis=0, tiled=True
        ),
    )
    coarse_idx = jnp.arange(count_ctx, dtype=jnp.int32)
    coarse_freq = jnp.arange(2 * count_ctx, dtype=jnp.int32)
    coarse_angle = angle_table(coarse_freq, coarse_idx, 2 * count_ctx)
    cos_coarse = jnp.cos(coarse_angle)
    sin_coarse = jnp.sin(coarse_angle)
    fine_global = my_index * sub_rows + jnp.arange(sub_rows, dtype=jnp.int32)
    twist_in = angle_table(coarse_freq, fine_global, period)
    source_re, source_im = section_coarse(
        got_source.astype(jnp.float32), cos_coarse, sin_coarse, twist_in
    )
    filter_re, filter_im = section_coarse(
        got_filter.astype(jnp.float32), cos_coarse, sin_coarse, twist_in
    )
    source_re, source_im, filter_re, filter_im = (
        lax.all_to_all(
            source_re.astype(jnp.bfloat16), CTX, split_axis=0, concat_axis=1, tiled=True
        ).astype(source_re.dtype),
        lax.all_to_all(
            source_im.astype(jnp.bfloat16), CTX, split_axis=0, concat_axis=1, tiled=True
        ).astype(source_im.dtype),
        lax.all_to_all(
            filter_re.astype(jnp.bfloat16), CTX, split_axis=0, concat_axis=1, tiled=True
        ).astype(filter_re.dtype),
        lax.all_to_all(
            filter_im.astype(jnp.bfloat16), CTX, split_axis=0, concat_axis=1, tiled=True
        ).astype(filter_im.dtype),
    )
    fine_idx = jnp.arange(tok_rows, dtype=jnp.int32)
    fine_angle = angle_table(fine_idx, fine_idx, tok_rows)
    cos_fine = jnp.cos(fine_angle)
    sin_fine = jnp.sin(fine_angle)
    source_re, source_im = section_fine(source_re, source_im, cos_fine, sin_fine, -1.0)
    filter_re, filter_im = section_fine(filter_re, filter_im, cos_fine, sin_fine, -1.0)
    split_re = source_re.reshape(2, tok_rows, groups, share)
    split_im = source_im.reshape(2, tok_rows, groups, share)
    prod_re = split_re * filter_re[..., None] - split_im * filter_im[..., None]
    prod_im = split_re * filter_im[..., None] + split_im * filter_re[..., None]
    back_re, back_im = section_fine(
        prod_re.reshape(2, tok_rows, chans),
        prod_im.reshape(2, tok_rows, chans),
        cos_fine,
        sin_fine,
        1.0,
    )
    pair_freq = my_index * 2 + jnp.arange(2, dtype=jnp.int32)
    twist_out = angle_table(pair_freq, fine_idx, period)
    cos_out = jnp.cos(twist_out)[:, :, None]
    sin_out = jnp.sin(twist_out)[:, :, None]
    turned_re = back_re * cos_out - back_im * sin_out
    turned_im = back_re * sin_out + back_im * cos_out
    turned_re, turned_im = (
        lax.all_to_all(
            turned_re.astype(jnp.bfloat16), CTX, split_axis=1, concat_axis=0, tiled=True
        ).astype(turned_re.dtype),
        lax.all_to_all(
            turned_im.astype(jnp.bfloat16), CTX, split_axis=1, concat_axis=0, tiled=True
        ).astype(turned_im.dtype),
    )
    result = jnp.einsum("nk,ksc->nsc", cos_coarse.T, turned_re, precision=highest)
    result = result - jnp.einsum("nk,ksc->nsc", sin_coarse.T, turned_im, precision=highest)
    rounded = (result / period).astype(jnp.bfloat16)
    returned = lax.all_to_all(rounded, CTX, split_axis=0, concat_axis=1, tiled=True)
    return returned.reshape(tok_rows, chans)


CTX = ("zh", "zl", "yh", "x")
HALF = ("zl", "yh", "x")


def flash_kernel(info_ref, q_ref, k_ref, v_ref, acc_ref, m_ref, l_ref, *, heads, tok_rows, key_block, scale):
    j = pl.program_id(0)
    q_first = info_ref[0]
    last_block = info_ref[1] - 1
    key_first = j * key_block

    @pl.when(j == 0)
    def _():
        m_ref[...] = jnp.full_like(m_ref, neg_large)
        l_ref[...] = jnp.zeros_like(l_ref)
        acc_ref[...] = jnp.zeros_like(acc_ref)

    def step(masked):
        if masked:
            query_pos = q_first + lax.broadcasted_iota(jnp.int32, (tok_rows, key_block), 0)
            key_pos = key_first + lax.broadcasted_iota(jnp.int32, (tok_rows, key_block), 1)
            allowed = key_pos <= query_pos
        for h in range(heads):
            cols = slice(h * HD, (h + 1) * HD)
            scores = lax.dot_general(
                q_ref[:, cols], k_ref[:, cols], (((1,), (1,)), ((), ())),
                preferred_element_type=jnp.float32,
            ) * scale
            if masked:
                scores = jnp.where(allowed, scores, neg_large)
            m_prev = m_ref[h]
            m_new = jnp.maximum(m_prev, jnp.max(scores, axis=1, keepdims=True))
            weights = jnp.exp(scores - m_new)
            if masked:
                weights = jnp.where(allowed, weights, 0.0)
            factor = jnp.exp(m_prev - m_new)
            l_ref[h] = l_ref[h] * factor + jnp.sum(weights, axis=1, keepdims=True)
            acc_ref[:, cols] = acc_ref[:, cols] * factor + jnp.dot(
                weights.astype(jnp.bfloat16), v_ref[:, cols], preferred_element_type=jnp.float32
            )
            m_ref[h] = m_new

    full = key_first + key_block <= q_first

    @pl.when(jnp.logical_and(j <= last_block, full))
    def _():
        step(False)

    @pl.when(jnp.logical_and(j <= last_block, jnp.logical_not(full)))
    def _():
        step(True)


def flash_partial(queries, keys, values, q_first, needed, key_block):
    tok_rows, width = queries.shape
    heads = width // HD
    total_rows = keys.shape[0]
    info = jnp.stack([q_first, needed]).astype(jnp.int32)
    kernel = partial(flash_kernel, heads=heads, tok_rows=tok_rows, key_block=key_block, scale=HD ** (-0.5))
    kv_spec = pl.BlockSpec((key_block, width), lambda j, info: (jnp.minimum(j, info[1] - 1), 0))
    stat_spec = pl.BlockSpec((heads, tok_rows, 1), lambda j, info: (0, 0, 0))
    return pl.pallas_call(
        kernel,
        out_shape=(
            jax.ShapeDtypeStruct((tok_rows, width), jnp.float32),
            jax.ShapeDtypeStruct((heads, tok_rows, 1), jnp.float32),
            jax.ShapeDtypeStruct((heads, tok_rows, 1), jnp.float32),
        ),
        grid_spec=pltpu.PrefetchScalarGridSpec(
            num_scalar_prefetch=1,
            grid=(total_rows // key_block,),
            in_specs=[pl.BlockSpec((tok_rows, width), lambda j, info: (0, 0)), kv_spec, kv_spec],
            out_specs=[pl.BlockSpec((tok_rows, width), lambda j, info: (0, 0)), stat_spec, stat_spec],
        ),
        compiler_params=pltpu.CompilerParams(
            dimension_semantics=("arbitrary",), vmem_limit_bytes=48 * 1024 * 1024
        ),
        cost_estimate=pl.CostEstimate(
            flops=4 * tok_rows * total_rows * width,
            transcendentals=heads * tok_rows * total_rows,
            bytes_accessed=2 * total_rows * width * 2 + tok_rows * width * 6,
        ),
    )(info, queries, keys, values)


def attention(q_attn, k_attn, v_attn, tok_rows):
    width = q_attn.shape[1]
    heads = width // HD
    upper = lax.axis_index("zh")
    half_count = 1
    for name in HALF:
        half_count = half_count * lax.axis_size(name)
    my_index = lax.axis_index(CTX)
    local_index = my_index - upper * half_count
    key_half = lax.all_gather(k_attn, HALF, axis=0, tiled=True)
    value_half = lax.all_gather(v_attn, HALF, axis=0, tiled=True)
    half_rows = key_half.shape[0]
    key_block = 896 if half_rows % 896 == 0 else tok_rows
    visiting = lax.ppermute(q_attn, "zh", [(1, 0)])
    cross = flash_partial(
        visiting, key_half, value_half, jnp.int32(half_rows), jnp.int32(half_rows // key_block), key_block
    )
    cross_acc, cross_max, cross_total = lax.ppermute(cross, "zh", [(0, 1)])
    needed = ((local_index + 1) * tok_rows + key_block - 1) // key_block
    own_acc, own_max, own_total = flash_partial(
        q_attn, key_half, value_half, local_index * tok_rows, needed, key_block
    )
    cross_max = jnp.where(upper == 0, neg_large, cross_max)
    top = jnp.maximum(own_max, cross_max)
    own_scale = jnp.exp(own_max - top)
    cross_scale = jnp.exp(cross_max - top)
    totals = own_total * own_scale + cross_total * cross_scale
    to_rows = lambda stat: stat.transpose(1, 0, 2)
    merged = (
        own_acc.reshape(tok_rows, heads, HD) * to_rows(own_scale)
        + cross_acc.reshape(tok_rows, heads, HD) * to_rows(cross_scale)
    ) / to_rows(totals)
    return merged.reshape(tok_rows, width).astype(jnp.bfloat16)


def local(q_conv, k_conv, v_conv, conv_filter, q_attn, k_attn, v_attn, w_conv_out, w_attn_out):
    count_ctx = lax.axis_size(CTX)
    my_index = lax.axis_index(CTX)
    tok_rows = q_conv.shape[0]
    gated = (k_conv.astype(jnp.float32) * v_conv.astype(jnp.float32)).astype(jnp.bfloat16)
    conv = spectral_conv(gated, conv_filter, my_index, tok_rows, count_ctx)
    mixed = (q_conv.astype(jnp.float32) * conv.astype(jnp.float32)).astype(jnp.bfloat16)
    attended = attention(q_attn, k_attn, v_attn, tok_rows)
    return lax.psum_scatter(
        (
            jnp.dot(mixed, w_conv_out, preferred_element_type=jnp.float32)
            + jnp.dot(attended, w_attn_out, preferred_element_type=jnp.float32)
        ).astype(jnp.bfloat16),
        "ch",
        scatter_dimension=0,
        tiled=True,
    )


def solution(mesh):
    ctx_size, ch_size = mesh.devices.shape
    split_mesh = jax.sharding.Mesh(
        mesh.devices.reshape(2, 2, 2, ctx_size // 8, ch_size), CTX + ("ch",)
    )
    tokens = P(CTX, "ch")
    return jax.shard_map(
        local,
        mesh=split_mesh,
        in_specs=(tokens,) * 7 + (P("ch", None), P("ch", None)),
        out_specs=P(CTX + ("ch",), None),
        check_vma=False,
    )
```

```python
from functools import partial
import math

import jax
import jax.numpy as jnp
from jax import lax
from jax.sharding import PartitionSpec as P
from jax.experimental import pallas as pl
from jax.experimental.pallas import tpu as pltpu

HD = 128


two_pi = 2.0 * math.pi
neg_large = -1e30
highest = lax.Precision.HIGHEST


def angle_table(left_idx, right_idx, period):
    product = left_idx[:, None] * right_idx[None, :] % period
    return product.astype(jnp.float32) * (two_pi / period)


def section_coarse(values, cos_table, sin_table, twiddle):
    real_part = jnp.einsum("kn,nsc->ksc", cos_table, values, precision=highest)
    imag_part = -jnp.einsum("kn,nsc->ksc", sin_table, values, precision=highest)
    cos_twist = jnp.cos(twiddle)[:, :, None]
    sin_twist = jnp.sin(twiddle)[:, :, None]
    return (
        real_part * cos_twist + imag_part * sin_twist,
        imag_part * cos_twist - real_part * sin_twist,
    )


def section_fine(real_part, imag_part, cos_table, sin_table, direction):
    cos_real = jnp.einsum("kn,anc->akc", cos_table, real_part, precision=highest)
    cos_imag = jnp.einsum("kn,anc->akc", cos_table, imag_part, precision=highest)
    sin_real = jnp.einsum("kn,anc->akc", sin_table, real_part, precision=highest)
    sin_imag = jnp.einsum("kn,anc->akc", sin_table, imag_part, precision=highest)
    return (cos_real - direction * sin_imag, cos_imag + direction * sin_real)


def spectral_conv(gated, filters, my_index, tok_rows, count_ctx):
    chans = gated.shape[1]
    groups = filters.shape[1]
    share = chans // groups
    sub_rows = tok_rows // count_ctx
    period = 2 * count_ctx * tok_rows
    both = lax.all_to_all(
        jnp.concatenate([gated, filters], axis=1).reshape(1, tok_rows, chans + groups),
        CTX, split_axis=1, concat_axis=0, tiled=True,
    )
    got_source = both[:, :, :chans]
    got_filter = both[:, :, chans:]
    coarse_idx = jnp.arange(count_ctx, dtype=jnp.int32)
    coarse_freq = jnp.arange(2 * count_ctx, dtype=jnp.int32)
    coarse_angle = angle_table(coarse_freq, coarse_idx, 2 * count_ctx)
    cos_coarse = jnp.cos(coarse_angle)
    sin_coarse = jnp.sin(coarse_angle)
    fine_global = my_index * sub_rows + jnp.arange(sub_rows, dtype=jnp.int32)
    twist_in = angle_table(coarse_freq, fine_global, period)
    source_re, source_im = section_coarse(
        got_source.astype(jnp.float32), cos_coarse, sin_coarse, twist_in
    )
    filter_re, filter_im = section_coarse(
        got_filter.astype(jnp.float32), cos_coarse, sin_coarse, twist_in
    )
    packed = lax.all_to_all(
        jnp.concatenate([source_re, source_im, filter_re, filter_im], axis=2).astype(jnp.bfloat16),
        CTX, split_axis=0, concat_axis=1, tiled=True,
    ).astype(jnp.float32)
    source_re = packed[:, :, :chans]
    source_im = packed[:, :, chans:2 * chans]
    filter_re = packed[:, :, 2 * chans:2 * chans + groups]
    filter_im = packed[:, :, 2 * chans + groups:]
    fine_idx = jnp.arange(tok_rows, dtype=jnp.int32)
    fine_angle = angle_table(fine_idx, fine_idx, tok_rows)
    cos_fine = jnp.cos(fine_angle)
    sin_fine = jnp.sin(fine_angle)
    source_re, source_im = section_fine(source_re, source_im, cos_fine, sin_fine, -1.0)
    filter_re, filter_im = section_fine(filter_re, filter_im, cos_fine, sin_fine, -1.0)
    split_re = source_re.reshape(2, tok_rows, groups, share)
    split_im = source_im.reshape(2, tok_rows, groups, share)
    prod_re = split_re * filter_re[..., None] - split_im * filter_im[..., None]
    prod_im = split_re * filter_im[..., None] + split_im * filter_re[..., None]
    back_re, back_im = section_fine(
        prod_re.reshape(2, tok_rows, chans),
        prod_im.reshape(2, tok_rows, chans),
        cos_fine,
        sin_fine,
        1.0,
    )
    pair_freq = my_index * 2 + jnp.arange(2, dtype=jnp.int32)
    twist_out = angle_table(pair_freq, fine_idx, period)
    cos_out = jnp.cos(twist_out)[:, :, None]
    sin_out = jnp.sin(twist_out)[:, :, None]
    turned_re = back_re * cos_out - back_im * sin_out
    turned_im = back_re * sin_out + back_im * cos_out
    turned = lax.all_to_all(
        jnp.concatenate([turned_re, turned_im], axis=2).astype(jnp.bfloat16),
        CTX, split_axis=1, concat_axis=0, tiled=True,
    ).astype(jnp.float32)
    turned_re = turned[:, :, :chans]
    turned_im = turned[:, :, chans:]
    result = jnp.einsum("nk,ksc->nsc", cos_coarse.T, turned_re, precision=highest)
    result = result - jnp.einsum("nk,ksc->nsc", sin_coarse.T, turned_im, precision=highest)
    rounded = (result / period).astype(jnp.bfloat16)
    returned = lax.all_to_all(rounded, CTX, split_axis=0, concat_axis=1, tiled=True)
    return returned.reshape(tok_rows, chans)


CTX = ("zh", "zl", "yh", "x")
HALF = ("zl", "yh", "x")


def flash_kernel(info_ref, q_ref, k_ref, v_ref, acc_ref, m_ref, l_ref, *, heads, tok_rows, key_block, scale):
    j = pl.program_id(0)
    q_first = info_ref[0]
    last_block = info_ref[1] - 1
    key_first = j * key_block

    @pl.when(j == 0)
    def _():
        m_ref[...] = jnp.full_like(m_ref, neg_large)
        l_ref[...] = jnp.zeros_like(l_ref)
        acc_ref[...] = jnp.zeros_like(acc_ref)

    def step(masked):
        if masked:
            query_pos = q_first + lax.broadcasted_iota(jnp.int32, (tok_rows, key_block), 0)
            key_pos = key_first + lax.broadcasted_iota(jnp.int32, (tok_rows, key_block), 1)
            allowed = key_pos <= query_pos
        for h in range(heads):
            cols = slice(h * HD, (h + 1) * HD)
            scores = lax.dot_general(
                q_ref[:, cols], k_ref[:, cols], (((1,), (1,)), ((), ())),
                preferred_element_type=jnp.float32,
            ) * scale
            if masked:
                scores = jnp.where(allowed, scores, neg_large)
            m_prev = m_ref[h]
            m_new = jnp.maximum(m_prev, jnp.max(scores, axis=1, keepdims=True))
            weights = jnp.exp(scores - m_new)
            if masked:
                weights = jnp.where(allowed, weights, 0.0)
            factor = jnp.exp(m_prev - m_new)
            l_ref[h] = l_ref[h] * factor + jnp.sum(weights, axis=1, keepdims=True)
            acc_ref[:, cols] = acc_ref[:, cols] * factor + jnp.dot(
                weights.astype(jnp.bfloat16), v_ref[:, cols], preferred_element_type=jnp.float32
            )
            m_ref[h] = m_new

    full = key_first + key_block <= q_first

    @pl.when(jnp.logical_and(j <= last_block, full))
    def _():
        step(False)

    @pl.when(jnp.logical_and(j <= last_block, jnp.logical_not(full)))
    def _():
        step(True)


def flash_partial(queries, keys, values, q_first, needed, key_block):
    tok_rows, width = queries.shape
    heads = width // HD
    total_rows = keys.shape[0]
    info = jnp.stack([q_first, needed]).astype(jnp.int32)
    kernel = partial(flash_kernel, heads=heads, tok_rows=tok_rows, key_block=key_block, scale=HD ** (-0.5))
    kv_spec = pl.BlockSpec((key_block, width), lambda j, info: (jnp.minimum(j, info[1] - 1), 0))
    stat_spec = pl.BlockSpec((heads, tok_rows, 1), lambda j, info: (0, 0, 0))
    return pl.pallas_call(
        kernel,
        out_shape=(
            jax.ShapeDtypeStruct((tok_rows, width), jnp.float32),
            jax.ShapeDtypeStruct((heads, tok_rows, 1), jnp.float32),
            jax.ShapeDtypeStruct((heads, tok_rows, 1), jnp.float32),
        ),
        grid_spec=pltpu.PrefetchScalarGridSpec(
            num_scalar_prefetch=1,
            grid=(total_rows // key_block,),
            in_specs=[pl.BlockSpec((tok_rows, width), lambda j, info: (0, 0)), kv_spec, kv_spec],
            out_specs=[pl.BlockSpec((tok_rows, width), lambda j, info: (0, 0)), stat_spec, stat_spec],
        ),
        compiler_params=pltpu.CompilerParams(
            dimension_semantics=("arbitrary",), vmem_limit_bytes=48 * 1024 * 1024
        ),
        cost_estimate=pl.CostEstimate(
            flops=4 * tok_rows * total_rows * width,
            transcendentals=heads * tok_rows * total_rows,
            bytes_accessed=2 * total_rows * width * 2 + tok_rows * width * 6,
        ),
    )(info, queries, keys, values)


def attention(q_attn, k_attn, v_attn, tok_rows):
    width = q_attn.shape[1]
    heads = width // HD
    upper = lax.axis_index("zh")
    half_count = 1
    for name in HALF:
        half_count = half_count * lax.axis_size(name)
    my_index = lax.axis_index(CTX)
    local_index = my_index - upper * half_count
    key_half = lax.all_gather(k_attn, HALF, axis=0, tiled=True)
    value_half = lax.all_gather(v_attn, HALF, axis=0, tiled=True)
    half_rows = key_half.shape[0]
    key_block = 896 if half_rows % 896 == 0 else tok_rows
    visiting = lax.ppermute(q_attn, "zh", [(1, 0)])
    cross = flash_partial(
        visiting, key_half, value_half, jnp.int32(half_rows), jnp.int32(half_rows // key_block), key_block
    )
    cross_acc, cross_max, cross_total = lax.ppermute(cross, "zh", [(0, 1)])
    needed = ((local_index + 1) * tok_rows + key_block - 1) // key_block
    own_acc, own_max, own_total = flash_partial(
        q_attn, key_half, value_half, local_index * tok_rows, needed, key_block
    )
    cross_max = jnp.where(upper == 0, neg_large, cross_max)
    top = jnp.maximum(own_max, cross_max)
    own_scale = jnp.exp(own_max - top)
    cross_scale = jnp.exp(cross_max - top)
    totals = own_total * own_scale + cross_total * cross_scale
    to_rows = lambda stat: stat.transpose(1, 0, 2)
    merged = (
        own_acc.reshape(tok_rows, heads, HD) * to_rows(own_scale)
        + cross_acc.reshape(tok_rows, heads, HD) * to_rows(cross_scale)
    ) / to_rows(totals)
    return merged.reshape(tok_rows, width).astype(jnp.bfloat16)


def local(q_conv, k_conv, v_conv, conv_filter, q_attn, k_attn, v_attn, w_conv_out, w_attn_out):
    count_ctx = lax.axis_size(CTX)
    my_index = lax.axis_index(CTX)
    tok_rows = q_conv.shape[0]
    gated = (k_conv.astype(jnp.float32) * v_conv.astype(jnp.float32)).astype(jnp.bfloat16)
    conv = spectral_conv(gated, conv_filter, my_index, tok_rows, count_ctx)
    mixed = (q_conv.astype(jnp.float32) * conv.astype(jnp.float32)).astype(jnp.bfloat16)
    attended = attention(q_attn, k_attn, v_attn, tok_rows)
    return lax.psum_scatter(
        (
            jnp.dot(mixed, w_conv_out, preferred_element_type=jnp.float32)
            + jnp.dot(attended, w_attn_out, preferred_element_type=jnp.float32)
        ).astype(jnp.bfloat16),
        "ch",
        scatter_dimension=0,
        tiled=True,
    )


def solution(mesh):
    ctx_size, ch_size = mesh.devices.shape
    split_mesh = jax.sharding.Mesh(
        mesh.devices.reshape(2, 2, 2, ctx_size // 8, ch_size), CTX + ("ch",)
    )
    tokens = P(CTX, "ch")
    return jax.shard_map(
        local,
        mesh=split_mesh,
        in_specs=(tokens,) * 7 + (P("ch", None), P("ch", None)),
        out_specs=P(CTX + ("ch",), None),
        check_vma=False,
    )
```

```python
from functools import partial
import math

import jax
import jax.numpy as jnp
from jax import lax
from jax.sharding import PartitionSpec as P
from jax.experimental import pallas as pl
from jax.experimental.pallas import tpu as pltpu

HD = 128


two_pi = 2.0 * math.pi
neg_large = -1e30
highest = lax.Precision.HIGHEST


def angle_table(left_idx, right_idx, period):
    product = left_idx[:, None] * right_idx[None, :] % period
    return product.astype(jnp.float32) * (two_pi / period)


def section_coarse(values, cos_table, sin_table, twiddle):
    real_part = jnp.einsum("kn,nsc->ksc", cos_table, values, precision=highest)
    imag_part = -jnp.einsum("kn,nsc->ksc", sin_table, values, precision=highest)
    cos_twist = jnp.cos(twiddle)[:, :, None]
    sin_twist = jnp.sin(twiddle)[:, :, None]
    return (
        real_part * cos_twist + imag_part * sin_twist,
        imag_part * cos_twist - real_part * sin_twist,
    )


def section_fine(real_part, imag_part, cos_table, sin_table, direction):
    cos_real = jnp.einsum("kn,anc->akc", cos_table, real_part, precision=highest)
    cos_imag = jnp.einsum("kn,anc->akc", cos_table, imag_part, precision=highest)
    sin_real = jnp.einsum("kn,anc->akc", sin_table, real_part, precision=highest)
    sin_imag = jnp.einsum("kn,anc->akc", sin_table, imag_part, precision=highest)
    return (cos_real - direction * sin_imag, cos_imag + direction * sin_real)


def spectral_conv(gated, filters, my_index, tok_rows, count_ctx):
    chans = gated.shape[1]
    groups = filters.shape[1]
    share = chans // groups
    sub_rows = tok_rows // count_ctx
    period = 2 * count_ctx * tok_rows
    both = lax.all_to_all(
        jnp.concatenate([gated, filters], axis=1).reshape(1, tok_rows, chans + groups),
        CTX, split_axis=1, concat_axis=0, tiled=True,
    )
    got_source = both[:, :, :chans]
    got_filter = both[:, :, chans:]
    coarse_idx = jnp.arange(count_ctx, dtype=jnp.int32)
    coarse_freq = jnp.arange(2 * count_ctx, dtype=jnp.int32)
    coarse_angle = angle_table(coarse_freq, coarse_idx, 2 * count_ctx)
    cos_coarse = jnp.cos(coarse_angle)
    sin_coarse = jnp.sin(coarse_angle)
    fine_global = my_index * sub_rows + jnp.arange(sub_rows, dtype=jnp.int32)
    twist_in = angle_table(coarse_freq, fine_global, period)
    source_re, source_im = section_coarse(
        got_source.astype(jnp.float32), cos_coarse, sin_coarse, twist_in
    )
    filter_re, filter_im = section_coarse(
        got_filter.astype(jnp.float32), cos_coarse, sin_coarse, twist_in
    )
    packed = lax.all_to_all(
        jnp.concatenate([source_re, source_im, filter_re, filter_im], axis=2).astype(jnp.bfloat16),
        CTX, split_axis=0, concat_axis=1, tiled=True,
    ).astype(jnp.float32)
    source_re = packed[:, :, :chans]
    source_im = packed[:, :, chans:2 * chans]
    filter_re = packed[:, :, 2 * chans:2 * chans + groups]
    filter_im = packed[:, :, 2 * chans + groups:]
    fine_idx = jnp.arange(tok_rows, dtype=jnp.int32)
    fine_angle = angle_table(fine_idx, fine_idx, tok_rows)
    cos_fine = jnp.cos(fine_angle)
    sin_fine = jnp.sin(fine_angle)
    source_re, source_im = section_fine(source_re, source_im, cos_fine, sin_fine, -1.0)
    filter_re, filter_im = section_fine(filter_re, filter_im, cos_fine, sin_fine, -1.0)
    split_re = source_re.reshape(2, tok_rows, groups, share)
    split_im = source_im.reshape(2, tok_rows, groups, share)
    prod_re = split_re * filter_re[..., None] - split_im * filter_im[..., None]
    prod_im = split_re * filter_im[..., None] + split_im * filter_re[..., None]
    back_re, back_im = section_fine(
        prod_re.reshape(2, tok_rows, chans),
        prod_im.reshape(2, tok_rows, chans),
        cos_fine,
        sin_fine,
        1.0,
    )
    pair_freq = my_index * 2 + jnp.arange(2, dtype=jnp.int32)
    twist_out = angle_table(pair_freq, fine_idx, period)
    cos_out = jnp.cos(twist_out)[:, :, None]
    sin_out = jnp.sin(twist_out)[:, :, None]
    turned_re = back_re * cos_out - back_im * sin_out
    turned_im = back_re * sin_out + back_im * cos_out
    turned = lax.all_to_all(
        jnp.concatenate([turned_re, turned_im], axis=2).astype(jnp.bfloat16),
        CTX, split_axis=1, concat_axis=0, tiled=True,
    ).astype(jnp.float32)
    turned_re = turned[:, :, :chans]
    turned_im = turned[:, :, chans:]
    result = jnp.einsum("nk,ksc->nsc", cos_coarse.T, turned_re, precision=highest)
    result = result - jnp.einsum("nk,ksc->nsc", sin_coarse.T, turned_im, precision=highest)
    rounded = (result / period).astype(jnp.bfloat16)
    returned = lax.all_to_all(rounded, CTX, split_axis=0, concat_axis=1, tiled=True)
    return returned.reshape(tok_rows, chans)


CTX = ("zh", "zl", "yh", "x")
HALF = ("zl", "yh", "x")


def flash_kernel(info_ref, q_ref, k_ref, v_ref, acc_ref, m_ref, l_ref, *, heads, tok_rows, key_block, scale):
    j = pl.program_id(0)
    q_first = info_ref[0]
    last_block = info_ref[1] - 1
    key_first = j * key_block

    @pl.when(j == 0)
    def _():
        m_ref[...] = jnp.full_like(m_ref, neg_large)
        l_ref[...] = jnp.zeros_like(l_ref)
        acc_ref[...] = jnp.zeros_like(acc_ref)

    def step(masked):
        if masked:
            query_pos = q_first + lax.broadcasted_iota(jnp.int32, (tok_rows, key_block), 0)
            key_pos = key_first + lax.broadcasted_iota(jnp.int32, (tok_rows, key_block), 1)
            allowed = key_pos <= query_pos
        for h in range(heads):
            cols = slice(h * HD, (h + 1) * HD)
            scores = lax.dot_general(
                q_ref[:, cols], k_ref[:, cols], (((1,), (1,)), ((), ())),
                preferred_element_type=jnp.float32,
            ) * scale
            if masked:
                scores = jnp.where(allowed, scores, neg_large)
            m_prev = m_ref[h]
            m_new = jnp.maximum(m_prev, jnp.max(scores, axis=1, keepdims=True))
            weights = jnp.exp(scores - m_new)
            if masked:
                weights = jnp.where(allowed, weights, 0.0)
            factor = jnp.exp(m_prev - m_new)
            l_ref[h] = l_ref[h] * factor + jnp.sum(weights, axis=1, keepdims=True)
            acc_ref[:, cols] = acc_ref[:, cols] * factor + jnp.dot(
                weights.astype(jnp.bfloat16), v_ref[:, cols], preferred_element_type=jnp.float32
            )
            m_ref[h] = m_new

    full = key_first + key_block <= q_first

    @pl.when(jnp.logical_and(j <= last_block, full))
    def _():
        step(False)

    @pl.when(jnp.logical_and(j <= last_block, jnp.logical_not(full)))
    def _():
        step(True)


def flash_partial(queries, keys, values, q_first, needed, key_block):
    tok_rows, width = queries.shape
    heads = width // HD
    total_rows = keys.shape[0]
    info = jnp.stack([q_first, needed]).astype(jnp.int32)
    kernel = partial(flash_kernel, heads=heads, tok_rows=tok_rows, key_block=key_block, scale=HD ** (-0.5))
    kv_spec = pl.BlockSpec((key_block, width), lambda j, info: (jnp.minimum(j, info[1] - 1), 0))
    stat_spec = pl.BlockSpec((heads, tok_rows, 1), lambda j, info: (0, 0, 0))
    return pl.pallas_call(
        kernel,
        out_shape=(
            jax.ShapeDtypeStruct((tok_rows, width), jnp.float32),
            jax.ShapeDtypeStruct((heads, tok_rows, 1), jnp.float32),
            jax.ShapeDtypeStruct((heads, tok_rows, 1), jnp.float32),
        ),
        grid_spec=pltpu.PrefetchScalarGridSpec(
            num_scalar_prefetch=1,
            grid=(total_rows // key_block,),
            in_specs=[pl.BlockSpec((tok_rows, width), lambda j, info: (0, 0)), kv_spec, kv_spec],
            out_specs=[pl.BlockSpec((tok_rows, width), lambda j, info: (0, 0)), stat_spec, stat_spec],
        ),
        compiler_params=pltpu.CompilerParams(
            dimension_semantics=("arbitrary",), vmem_limit_bytes=48 * 1024 * 1024
        ),
        cost_estimate=pl.CostEstimate(
            flops=4 * tok_rows * total_rows * width,
            transcendentals=heads * tok_rows * total_rows,
            bytes_accessed=2 * total_rows * width * 2 + tok_rows * width * 6,
        ),
    )(info, queries, keys, values)


def attention(q_attn, k_attn, v_attn, tok_rows):
    width = q_attn.shape[1]
    heads = width // HD
    upper = lax.axis_index("zh")
    half_count = 1
    for name in HALF:
        half_count = half_count * lax.axis_size(name)
    my_index = lax.axis_index(CTX)
    local_index = my_index - upper * half_count
    key_half = lax.all_gather(k_attn, HALF, axis=0, tiled=True)
    value_half = lax.all_gather(v_attn, HALF, axis=0, tiled=True)
    half_rows = key_half.shape[0]
    key_block = 896 if half_rows % 896 == 0 else tok_rows
    visiting = lax.ppermute(q_attn, "zh", [(1, 0)])
    cross = flash_partial(
        visiting, key_half, value_half, jnp.int32(half_rows), jnp.int32(half_rows // key_block), key_block
    )
    stats = jnp.concatenate([cross[1].reshape(heads, tok_rows), cross[2].reshape(heads, tok_rows)])
    cross_acc, cross_stats = lax.ppermute((cross[0], stats), "zh", [(0, 1)])
    cross_max = cross_stats[:heads].reshape(heads, tok_rows, 1)
    cross_total = cross_stats[heads:].reshape(heads, tok_rows, 1)
    needed = ((local_index + 1) * tok_rows + key_block - 1) // key_block
    own_acc, own_max, own_total = flash_partial(
        q_attn, key_half, value_half, local_index * tok_rows, needed, key_block
    )
    cross_max = jnp.where(upper == 0, neg_large, cross_max)
    top = jnp.maximum(own_max, cross_max)
    own_scale = jnp.exp(own_max - top)
    cross_scale = jnp.exp(cross_max - top)
    totals = own_total * own_scale + cross_total * cross_scale
    to_rows = lambda stat: stat.transpose(1, 0, 2)
    merged = (
        own_acc.reshape(tok_rows, heads, HD) * to_rows(own_scale)
        + cross_acc.reshape(tok_rows, heads, HD) * to_rows(cross_scale)
    ) / to_rows(totals)
    return merged.reshape(tok_rows, width).astype(jnp.bfloat16)


def local(q_conv, k_conv, v_conv, conv_filter, q_attn, k_attn, v_attn, w_conv_out, w_attn_out):
    count_ctx = lax.axis_size(CTX)
    my_index = lax.axis_index(CTX)
    tok_rows = q_conv.shape[0]
    gated = (k_conv.astype(jnp.float32) * v_conv.astype(jnp.float32)).astype(jnp.bfloat16)
    conv = spectral_conv(gated, conv_filter, my_index, tok_rows, count_ctx)
    mixed = (q_conv.astype(jnp.float32) * conv.astype(jnp.float32)).astype(jnp.bfloat16)
    attended = attention(q_attn, k_attn, v_attn, tok_rows)
    return lax.psum_scatter(
        (
            jnp.dot(mixed, w_conv_out, preferred_element_type=jnp.float32)
            + jnp.dot(attended, w_attn_out, preferred_element_type=jnp.float32)
        ).astype(jnp.bfloat16),
        "ch",
        scatter_dimension=0,
        tiled=True,
    )


def solution(mesh):
    ctx_size, ch_size = mesh.devices.shape
    split_mesh = jax.sharding.Mesh(
        mesh.devices.reshape(2, 2, 2, ctx_size // 8, ch_size), CTX + ("ch",)
    )
    tokens = P(CTX, "ch")
    return jax.shard_map(
        local,
        mesh=split_mesh,
        in_specs=(tokens,) * 7 + (P("ch", None), P("ch", None)),
        out_specs=P(CTX + ("ch",), None),
        check_vma=False,
    )
```

```python
from functools import partial
import math

import jax
import jax.numpy as jnp
from jax import lax
from jax.sharding import PartitionSpec as P
from jax.experimental import pallas as pl
from jax.experimental.pallas import tpu as pltpu

HD = 128


two_pi = 2.0 * math.pi
neg_large = -1e30
highest = lax.Precision.HIGHEST


def angle_table(left_idx, right_idx, period):
    product = left_idx[:, None] * right_idx[None, :] % period
    return product.astype(jnp.float32) * (two_pi / period)


def section_coarse(values, cos_table, sin_table, twiddle):
    real_part = jnp.einsum("kn,nsc->ksc", cos_table, values, precision=highest)
    imag_part = -jnp.einsum("kn,nsc->ksc", sin_table, values, precision=highest)
    cos_twist = jnp.cos(twiddle)[:, :, None]
    sin_twist = jnp.sin(twiddle)[:, :, None]
    return (
        real_part * cos_twist + imag_part * sin_twist,
        imag_part * cos_twist - real_part * sin_twist,
    )


def section_fine(real_part, imag_part, cos_table, sin_table, direction):
    cos_real = jnp.einsum("kn,anc->akc", cos_table, real_part, precision=highest)
    cos_imag = jnp.einsum("kn,anc->akc", cos_table, imag_part, precision=highest)
    sin_real = jnp.einsum("kn,anc->akc", sin_table, real_part, precision=highest)
    sin_imag = jnp.einsum("kn,anc->akc", sin_table, imag_part, precision=highest)
    return (cos_real - direction * sin_imag, cos_imag + direction * sin_real)


def spectral_conv(gated, filters, my_index, tok_rows, count_ctx):
    chans = gated.shape[1]
    groups = filters.shape[1]
    share = chans // groups
    sub_rows = tok_rows // count_ctx
    period = 2 * count_ctx * tok_rows
    both = lax.all_to_all(
        jnp.concatenate([gated, filters], axis=1).reshape(1, tok_rows, chans + groups),
        CTX, split_axis=1, concat_axis=0, tiled=True,
    )
    got_source = both[:, :, :chans]
    got_filter = both[:, :, chans:]
    coarse_idx = jnp.arange(count_ctx, dtype=jnp.int32)
    coarse_freq = jnp.arange(2 * count_ctx, dtype=jnp.int32)
    coarse_angle = angle_table(coarse_freq, coarse_idx, 2 * count_ctx)
    cos_coarse = jnp.cos(coarse_angle)
    sin_coarse = jnp.sin(coarse_angle)
    fine_global = my_index * sub_rows + jnp.arange(sub_rows, dtype=jnp.int32)
    twist_in = angle_table(coarse_freq, fine_global, period)
    source_re, source_im = section_coarse(
        got_source.astype(jnp.float32), cos_coarse, sin_coarse, twist_in
    )
    filter_re, filter_im = section_coarse(
        got_filter.astype(jnp.float32), cos_coarse, sin_coarse, twist_in
    )
    packed = lax.all_to_all(
        jnp.concatenate([source_re, source_im, filter_re, filter_im], axis=2).astype(jnp.bfloat16),
        CTX, split_axis=0, concat_axis=1, tiled=True,
    ).astype(jnp.float32)
    source_re = packed[:, :, :chans]
    source_im = packed[:, :, chans:2 * chans]
    filter_re = packed[:, :, 2 * chans:2 * chans + groups]
    filter_im = packed[:, :, 2 * chans + groups:]
    fine_idx = jnp.arange(tok_rows, dtype=jnp.int32)
    fine_angle = angle_table(fine_idx, fine_idx, tok_rows)
    cos_fine = jnp.cos(fine_angle)
    sin_fine = jnp.sin(fine_angle)
    source_re, source_im = section_fine(source_re, source_im, cos_fine, sin_fine, -1.0)
    filter_re, filter_im = section_fine(filter_re, filter_im, cos_fine, sin_fine, -1.0)
    split_re = source_re.reshape(2, tok_rows, groups, share)
    split_im = source_im.reshape(2, tok_rows, groups, share)
    prod_re = split_re * filter_re[..., None] - split_im * filter_im[..., None]
    prod_im = split_re * filter_im[..., None] + split_im * filter_re[..., None]
    back_re, back_im = section_fine(
        prod_re.reshape(2, tok_rows, chans),
        prod_im.reshape(2, tok_rows, chans),
        cos_fine,
        sin_fine,
        1.0,
    )
    pair_freq = my_index * 2 + jnp.arange(2, dtype=jnp.int32)
    twist_out = angle_table(pair_freq, fine_idx, period)
    cos_out = jnp.cos(twist_out)[:, :, None]
    sin_out = jnp.sin(twist_out)[:, :, None]
    turned_re = back_re * cos_out - back_im * sin_out
    turned_im = back_re * sin_out + back_im * cos_out
    turned = lax.all_to_all(
        jnp.concatenate([turned_re, turned_im], axis=2).astype(jnp.bfloat16),
        CTX, split_axis=1, concat_axis=0, tiled=True,
    ).astype(jnp.float32)
    turned_re = turned[:, :, :chans]
    turned_im = turned[:, :, chans:]
    result = jnp.einsum("nk,ksc->nsc", cos_coarse.T, turned_re, precision=highest)
    result = result - jnp.einsum("nk,ksc->nsc", sin_coarse.T, turned_im, precision=highest)
    rounded = (result / period).astype(jnp.bfloat16)
    returned = lax.all_to_all(rounded, CTX, split_axis=0, concat_axis=1, tiled=True)
    return returned.reshape(tok_rows, chans)


CTX = ("z", "yh", "x")
HALF = ("yh", "x")


def flash_kernel(info_ref, q_ref, k_ref, v_ref, acc_ref, m_ref, l_ref, *, heads, tok_rows, key_block, scale):
    j = pl.program_id(0)
    q_first = info_ref[0]
    last_block = info_ref[1] - 1
    key_first = j * key_block

    @pl.when(j == 0)
    def _():
        m_ref[...] = jnp.full_like(m_ref, neg_large)
        l_ref[...] = jnp.zeros_like(l_ref)
        acc_ref[...] = jnp.zeros_like(acc_ref)

    def step(masked):
        if masked:
            query_pos = q_first + lax.broadcasted_iota(jnp.int32, (tok_rows, key_block), 0)
            key_pos = key_first + lax.broadcasted_iota(jnp.int32, (tok_rows, key_block), 1)
            allowed = key_pos <= query_pos
        for h in range(heads):
            cols = slice(h * HD, (h + 1) * HD)
            scores = lax.dot_general(
                q_ref[:, cols], k_ref[:, cols], (((1,), (1,)), ((), ())),
                preferred_element_type=jnp.float32,
            ) * scale
            if masked:
                scores = jnp.where(allowed, scores, neg_large)
            m_prev = m_ref[h]
            m_new = jnp.maximum(m_prev, jnp.max(scores, axis=1, keepdims=True))
            weights = jnp.exp(scores - m_new)
            if masked:
                weights = jnp.where(allowed, weights, 0.0)
            factor = jnp.exp(m_prev - m_new)
            l_ref[h] = l_ref[h] * factor + jnp.sum(weights, axis=1, keepdims=True)
            acc_ref[:, cols] = acc_ref[:, cols] * factor + jnp.dot(
                weights.astype(jnp.bfloat16), v_ref[:, cols], preferred_element_type=jnp.float32
            )
            m_ref[h] = m_new

    full = key_first + key_block <= q_first

    @pl.when(jnp.logical_and(j <= last_block, full))
    def _():
        step(False)

    @pl.when(jnp.logical_and(j <= last_block, jnp.logical_not(full)))
    def _():
        step(True)


def flash_partial(queries, keys, values, q_first, needed, key_block):
    tok_rows, width = queries.shape
    heads = width // HD
    total_rows = keys.shape[0]
    info = jnp.stack([q_first, needed]).astype(jnp.int32)
    kernel = partial(flash_kernel, heads=heads, tok_rows=tok_rows, key_block=key_block, scale=HD ** (-0.5))
    kv_spec = pl.BlockSpec((key_block, width), lambda j, info: (jnp.minimum(j, info[1] - 1), 0))
    stat_spec = pl.BlockSpec((heads, tok_rows, 1), lambda j, info: (0, 0, 0))
    return pl.pallas_call(
        kernel,
        out_shape=(
            jax.ShapeDtypeStruct((tok_rows, width), jnp.float32),
            jax.ShapeDtypeStruct((heads, tok_rows, 1), jnp.float32),
            jax.ShapeDtypeStruct((heads, tok_rows, 1), jnp.float32),
        ),
        grid_spec=pltpu.PrefetchScalarGridSpec(
            num_scalar_prefetch=1,
            grid=(total_rows // key_block,),
            in_specs=[pl.BlockSpec((tok_rows, width), lambda j, info: (0, 0)), kv_spec, kv_spec],
            out_specs=[pl.BlockSpec((tok_rows, width), lambda j, info: (0, 0)), stat_spec, stat_spec],
        ),
        compiler_params=pltpu.CompilerParams(
            dimension_semantics=("arbitrary",), vmem_limit_bytes=48 * 1024 * 1024
        ),
        cost_estimate=pl.CostEstimate(
            flops=4 * tok_rows * total_rows * width,
            transcendentals=heads * tok_rows * total_rows,
            bytes_accessed=2 * total_rows * width * 2 + tok_rows * width * 6,
        ),
    )(info, queries, keys, values)


def attention(q_attn, k_attn, v_attn, tok_rows):
    width = q_attn.shape[1]
    heads = width // HD
    quarters = lax.axis_size("z")
    quarter = lax.axis_index("z")
    half_count = 1
    for name in HALF:
        half_count = half_count * lax.axis_size(name)
    my_index = lax.axis_index(CTX)
    local_index = my_index - quarter * half_count
    key_part = lax.all_gather(k_attn, HALF, axis=0, tiled=True)
    value_part = lax.all_gather(v_attn, HALF, axis=0, tiled=True)
    part_rows = key_part.shape[0]
    key_block = 896 if part_rows % 896 == 0 else tok_rows
    states = []
    for shift in range(1, quarters):
        visiting = lax.ppermute(q_attn, "z", [(k, k - shift) for k in range(shift, quarters)])
        cross = flash_partial(
            visiting, key_part, value_part, jnp.int32(part_rows), jnp.int32(part_rows // key_block), key_block
        )
        stats = jnp.concatenate([cross[1].reshape(heads, tok_rows), cross[2].reshape(heads, tok_rows)])
        back_acc, back_stats = lax.ppermute(
            (cross[0], stats), "z", [(k - shift, k) for k in range(shift, quarters)]
        )
        back_max = jnp.where(quarter >= shift, back_stats[:heads], neg_large)
        states.append((back_acc, back_max, back_stats[heads:]))
    needed = ((local_index + 1) * tok_rows + key_block - 1) // key_block
    own_acc, own_max, own_total = flash_partial(
        q_attn, key_part, value_part, local_index * tok_rows, needed, key_block
    )
    states.append((own_acc, own_max.reshape(heads, tok_rows), own_total.reshape(heads, tok_rows)))
    top = states[0][1]
    for state in states[1:]:
        top = jnp.maximum(top, state[1])
    merged = None
    totals = None
    for acc, row_max, row_total in states:
        scale = jnp.exp(row_max - top)
        part = acc.reshape(tok_rows, heads, HD) * scale.T[:, :, None]
        merged = part if merged is None else merged + part
        totals = scale * row_total if totals is None else totals + scale * row_total
    merged = merged / totals.T[:, :, None]
    return merged.reshape(tok_rows, width).astype(jnp.bfloat16)


def local(q_conv, k_conv, v_conv, conv_filter, q_attn, k_attn, v_attn, w_conv_out, w_attn_out):
    count_ctx = lax.axis_size(CTX)
    my_index = lax.axis_index(CTX)
    tok_rows = q_conv.shape[0]
    gated = (k_conv.astype(jnp.float32) * v_conv.astype(jnp.float32)).astype(jnp.bfloat16)
    conv = spectral_conv(gated, conv_filter, my_index, tok_rows, count_ctx)
    mixed = (q_conv.astype(jnp.float32) * conv.astype(jnp.float32)).astype(jnp.bfloat16)
    attended = attention(q_attn, k_attn, v_attn, tok_rows)
    return lax.psum_scatter(
        (
            jnp.dot(mixed, w_conv_out, preferred_element_type=jnp.float32)
            + jnp.dot(attended, w_attn_out, preferred_element_type=jnp.float32)
        ).astype(jnp.bfloat16),
        "ch",
        scatter_dimension=0,
        tiled=True,
    )


def solution(mesh):
    ctx_size, ch_size = mesh.devices.shape
    split_mesh = jax.sharding.Mesh(
        mesh.devices.reshape(ctx_size // 8, 2, 4, ch_size), CTX + ("ch",)
    )
    tokens = P(CTX, "ch")
    return jax.shard_map(
        local,
        mesh=split_mesh,
        in_specs=(tokens,) * 7 + (P("ch", None), P("ch", None)),
        out_specs=P(CTX + ("ch",), None),
        check_vma=False,
    )
```

```python
from functools import partial
import math

import jax
import jax.numpy as jnp
from jax import lax
from jax.sharding import PartitionSpec as P
from jax.experimental import pallas as pl
from jax.experimental.pallas import tpu as pltpu

HD = 128


two_pi = 2.0 * math.pi
neg_large = -1e30
highest = lax.Precision.HIGHEST


def angle_table(left_idx, right_idx, period):
    product = left_idx[:, None] * right_idx[None, :] % period
    return product.astype(jnp.float32) * (two_pi / period)


def section_coarse(values, cos_table, sin_table, twiddle):
    real_part = jnp.einsum("kn,nsc->ksc", cos_table, values, precision=highest)
    imag_part = -jnp.einsum("kn,nsc->ksc", sin_table, values, precision=highest)
    cos_twist = jnp.cos(twiddle)[:, :, None]
    sin_twist = jnp.sin(twiddle)[:, :, None]
    return (
        real_part * cos_twist + imag_part * sin_twist,
        imag_part * cos_twist - real_part * sin_twist,
    )


def section_fine(real_part, imag_part, cos_table, sin_table, direction):
    cos_real = jnp.einsum("kn,anc->akc", cos_table, real_part, precision=highest)
    cos_imag = jnp.einsum("kn,anc->akc", cos_table, imag_part, precision=highest)
    sin_real = jnp.einsum("kn,anc->akc", sin_table, real_part, precision=highest)
    sin_imag = jnp.einsum("kn,anc->akc", sin_table, imag_part, precision=highest)
    return (cos_real - direction * sin_imag, cos_imag + direction * sin_real)


def spectral_conv(gated, filters, my_index, tok_rows, count_ctx):
    chans = gated.shape[1]
    groups = filters.shape[1]
    share = chans // groups
    sub_rows = tok_rows // count_ctx
    period = 2 * count_ctx * tok_rows
    both = lax.all_to_all(
        jnp.concatenate([gated, filters], axis=1).reshape(1, tok_rows, chans + groups),
        CTX, split_axis=1, concat_axis=0, tiled=True,
    )
    got_source = both[:, :, :chans]
    got_filter = both[:, :, chans:]
    coarse_idx = jnp.arange(count_ctx, dtype=jnp.int32)
    coarse_freq = jnp.arange(2 * count_ctx, dtype=jnp.int32)
    coarse_angle = angle_table(coarse_freq, coarse_idx, 2 * count_ctx)
    cos_coarse = jnp.cos(coarse_angle)
    sin_coarse = jnp.sin(coarse_angle)
    fine_global = my_index * sub_rows + jnp.arange(sub_rows, dtype=jnp.int32)
    twist_in = angle_table(coarse_freq, fine_global, period)
    source_re, source_im = section_coarse(
        got_source.astype(jnp.float32), cos_coarse, sin_coarse, twist_in
    )
    filter_re, filter_im = section_coarse(
        got_filter.astype(jnp.float32), cos_coarse, sin_coarse, twist_in
    )
    packed = lax.all_to_all(
        jnp.concatenate([source_re, source_im, filter_re, filter_im], axis=2).astype(jnp.bfloat16),
        CTX, split_axis=0, concat_axis=1, tiled=True,
    ).astype(jnp.float32)
    source_re = packed[:, :, :chans]
    source_im = packed[:, :, chans:2 * chans]
    filter_re = packed[:, :, 2 * chans:2 * chans + groups]
    filter_im = packed[:, :, 2 * chans + groups:]
    fine_idx = jnp.arange(tok_rows, dtype=jnp.int32)
    fine_angle = angle_table(fine_idx, fine_idx, tok_rows)
    cos_fine = jnp.cos(fine_angle)
    sin_fine = jnp.sin(fine_angle)
    source_re, source_im = section_fine(source_re, source_im, cos_fine, sin_fine, -1.0)
    filter_re, filter_im = section_fine(filter_re, filter_im, cos_fine, sin_fine, -1.0)
    split_re = source_re.reshape(2, tok_rows, groups, share)
    split_im = source_im.reshape(2, tok_rows, groups, share)
    prod_re = split_re * filter_re[..., None] - split_im * filter_im[..., None]
    prod_im = split_re * filter_im[..., None] + split_im * filter_re[..., None]
    back_re, back_im = section_fine(
        prod_re.reshape(2, tok_rows, chans),
        prod_im.reshape(2, tok_rows, chans),
        cos_fine,
        sin_fine,
        1.0,
    )
    pair_freq = my_index * 2 + jnp.arange(2, dtype=jnp.int32)
    twist_out = angle_table(pair_freq, fine_idx, period)
    cos_out = jnp.cos(twist_out)[:, :, None]
    sin_out = jnp.sin(twist_out)[:, :, None]
    turned_re = back_re * cos_out - back_im * sin_out
    turned_im = back_re * sin_out + back_im * cos_out
    turned = lax.all_to_all(
        jnp.concatenate([turned_re, turned_im], axis=2).astype(jnp.bfloat16),
        CTX, split_axis=1, concat_axis=0, tiled=True,
    ).astype(jnp.float32)
    turned_re = turned[:, :, :chans]
    turned_im = turned[:, :, chans:]
    result = jnp.einsum("nk,ksc->nsc", cos_coarse.T, turned_re, precision=highest)
    result = result - jnp.einsum("nk,ksc->nsc", sin_coarse.T, turned_im, precision=highest)
    rounded = (result / period).astype(jnp.bfloat16)
    returned = lax.all_to_all(rounded, CTX, split_axis=0, concat_axis=1, tiled=True)
    return returned.reshape(tok_rows, chans)


CTX = ("z", "yh", "x")
EXP2_SCALE = math.log2(math.e) * HD ** (-0.5)
HALF = ("yh", "x")


def flash_kernel(info_ref, q_ref, k_ref, v_ref, acc_ref, m_ref, l_ref, *, heads, tok_rows, key_block, scale):
    j = pl.program_id(0)
    q_first = info_ref[0]
    last_block = info_ref[1] - 1
    key_first = j * key_block

    @pl.when(j == 0)
    def _():
        m_ref[...] = jnp.full_like(m_ref, neg_large)
        l_ref[...] = jnp.zeros_like(l_ref)
        acc_ref[...] = jnp.zeros_like(acc_ref)

    def step(masked):
        if masked:
            query_pos = q_first + lax.broadcasted_iota(jnp.int32, (tok_rows, key_block), 0)
            key_pos = key_first + lax.broadcasted_iota(jnp.int32, (tok_rows, key_block), 1)
            allowed = key_pos <= query_pos
        for h in range(heads):
            cols = slice(h * HD, (h + 1) * HD)
            scores = lax.dot_general(
                q_ref[:, cols], k_ref[:, cols], (((1,), (1,)), ((), ())),
                preferred_element_type=jnp.float32,
            )
            if masked:
                scores = jnp.where(allowed, scores, neg_large)
            m_prev = m_ref[h]
            m_new = jnp.maximum(m_prev, jnp.max(scores, axis=1, keepdims=True))
            weights = jnp.exp2((scores - m_new) * scale)
            if masked:
                weights = jnp.where(allowed, weights, 0.0)
            factor = jnp.exp2((m_prev - m_new) * scale)
            l_ref[h] = l_ref[h] * factor + jnp.sum(weights, axis=1, keepdims=True)
            acc_ref[:, cols] = acc_ref[:, cols] * factor + jnp.dot(
                weights.astype(jnp.bfloat16), v_ref[:, cols], preferred_element_type=jnp.float32
            )
            m_ref[h] = m_new

    full = key_first + key_block <= q_first

    @pl.when(jnp.logical_and(j <= last_block, full))
    def _():
        step(False)

    @pl.when(jnp.logical_and(j <= last_block, jnp.logical_not(full)))
    def _():
        step(True)


def flash_partial(queries, keys, values, q_first, needed, key_block):
    tok_rows, width = queries.shape
    heads = width // HD
    total_rows = keys.shape[0]
    info = jnp.stack([q_first, needed]).astype(jnp.int32)
    kernel = partial(flash_kernel, heads=heads, tok_rows=tok_rows, key_block=key_block, scale=EXP2_SCALE)
    kv_spec = pl.BlockSpec((key_block, width), lambda j, info: (jnp.minimum(j, info[1] - 1), 0))
    stat_spec = pl.BlockSpec((heads, tok_rows, 1), lambda j, info: (0, 0, 0))
    return pl.pallas_call(
        kernel,
        out_shape=(
            jax.ShapeDtypeStruct((tok_rows, width), jnp.float32),
            jax.ShapeDtypeStruct((heads, tok_rows, 1), jnp.float32),
            jax.ShapeDtypeStruct((heads, tok_rows, 1), jnp.float32),
        ),
        grid_spec=pltpu.PrefetchScalarGridSpec(
            num_scalar_prefetch=1,
            grid=(total_rows // key_block,),
            in_specs=[pl.BlockSpec((tok_rows, width), lambda j, info: (0, 0)), kv_spec, kv_spec],
            out_specs=[pl.BlockSpec((tok_rows, width), lambda j, info: (0, 0)), stat_spec, stat_spec],
        ),
        compiler_params=pltpu.CompilerParams(
            dimension_semantics=("arbitrary",), vmem_limit_bytes=48 * 1024 * 1024
        ),
        cost_estimate=pl.CostEstimate(
            flops=4 * tok_rows * total_rows * width,
            transcendentals=heads * tok_rows * total_rows,
            bytes_accessed=2 * total_rows * width * 2 + tok_rows * width * 6,
        ),
    )(info, queries, keys, values)


def attention(q_attn, k_attn, v_attn, tok_rows):
    width = q_attn.shape[1]
    heads = width // HD
    quarters = lax.axis_size("z")
    quarter = lax.axis_index("z")
    half_count = 1
    for name in HALF:
        half_count = half_count * lax.axis_size(name)
    my_index = lax.axis_index(CTX)
    local_index = my_index - quarter * half_count
    key_part = lax.all_gather(k_attn, HALF, axis=0, tiled=True)
    value_part = lax.all_gather(v_attn, HALF, axis=0, tiled=True)
    part_rows = key_part.shape[0]
    key_block = 896 if part_rows % 896 == 0 else tok_rows
    states = []
    for shift in range(1, quarters):
        visiting = lax.ppermute(q_attn, "z", [(k, k - shift) for k in range(shift, quarters)])
        cross = flash_partial(
            visiting, key_part, value_part, jnp.int32(part_rows), jnp.int32(part_rows // key_block), key_block
        )
        stats = jnp.concatenate([cross[1].reshape(heads, tok_rows), cross[2].reshape(heads, tok_rows)])
        back_acc, back_stats = lax.ppermute(
            (cross[0], stats), "z", [(k - shift, k) for k in range(shift, quarters)]
        )
        back_max = jnp.where(quarter >= shift, back_stats[:heads], neg_large)
        states.append((back_acc, back_max, back_stats[heads:]))
    needed = ((local_index + 1) * tok_rows + key_block - 1) // key_block
    own_acc, own_max, own_total = flash_partial(
        q_attn, key_part, value_part, local_index * tok_rows, needed, key_block
    )
    states.append((own_acc, own_max.reshape(heads, tok_rows), own_total.reshape(heads, tok_rows)))
    top = states[0][1]
    for state in states[1:]:
        top = jnp.maximum(top, state[1])
    merged = None
    totals = None
    for acc, row_max, row_total in states:
        scale = jnp.exp2((row_max - top) * EXP2_SCALE)
        part = acc.reshape(tok_rows, heads, HD) * scale.T[:, :, None]
        merged = part if merged is None else merged + part
        totals = scale * row_total if totals is None else totals + scale * row_total
    merged = merged / totals.T[:, :, None]
    return merged.reshape(tok_rows, width).astype(jnp.bfloat16)


def local(q_conv, k_conv, v_conv, conv_filter, q_attn, k_attn, v_attn, w_conv_out, w_attn_out):
    count_ctx = lax.axis_size(CTX)
    my_index = lax.axis_index(CTX)
    tok_rows = q_conv.shape[0]
    gated = (k_conv.astype(jnp.float32) * v_conv.astype(jnp.float32)).astype(jnp.bfloat16)
    conv = spectral_conv(gated, conv_filter, my_index, tok_rows, count_ctx)
    mixed = (q_conv.astype(jnp.float32) * conv.astype(jnp.float32)).astype(jnp.bfloat16)
    conv_part = jnp.dot(mixed, w_conv_out, preferred_element_type=jnp.float32)
    attended = attention(q_attn, k_attn, v_attn, tok_rows)
    return lax.psum_scatter(
        (conv_part + jnp.dot(attended, w_attn_out, preferred_element_type=jnp.float32)).astype(jnp.bfloat16),
        "ch",
        scatter_dimension=0,
        tiled=True,
    )


def solution(mesh):
    ctx_size, ch_size = mesh.devices.shape
    split_mesh = jax.sharding.Mesh(
        mesh.devices.reshape(ctx_size // 8, 2, 4, ch_size), CTX + ("ch",)
    )
    tokens = P(CTX, "ch")
    return jax.shard_map(
        local,
        mesh=split_mesh,
        in_specs=(tokens,) * 7 + (P("ch", None), P("ch", None)),
        out_specs=P(CTX + ("ch",), None),
        check_vma=False,
    )
```

```python
from functools import partial
import math

import jax
import jax.numpy as jnp
from jax import lax
from jax.sharding import PartitionSpec as P
from jax.experimental import pallas as pl
from jax.experimental.pallas import tpu as pltpu

HD = 128


two_pi = 2.0 * math.pi
neg_large = -1e30
highest = lax.Precision.HIGHEST


def angle_table(left_idx, right_idx, period):
    product = left_idx[:, None] * right_idx[None, :] % period
    return product.astype(jnp.float32) * (two_pi / period)


def section_coarse(values, cos_table, sin_table, twiddle):
    real_part = jnp.einsum("kn,nsc->ksc", cos_table, values, precision=highest)
    imag_part = -jnp.einsum("kn,nsc->ksc", sin_table, values, precision=highest)
    cos_twist = jnp.cos(twiddle)[:, :, None]
    sin_twist = jnp.sin(twiddle)[:, :, None]
    return (
        real_part * cos_twist + imag_part * sin_twist,
        imag_part * cos_twist - real_part * sin_twist,
    )


def section_fine(real_part, imag_part, cos_table, sin_table, direction):
    cos_real = jnp.einsum("kn,anc->akc", cos_table, real_part, precision=highest)
    cos_imag = jnp.einsum("kn,anc->akc", cos_table, imag_part, precision=highest)
    sin_real = jnp.einsum("kn,anc->akc", sin_table, real_part, precision=highest)
    sin_imag = jnp.einsum("kn,anc->akc", sin_table, imag_part, precision=highest)
    return (cos_real - direction * sin_imag, cos_imag + direction * sin_real)


def spectral_conv(gated, filters, my_index, tok_rows, count_ctx):
    chans = gated.shape[1]
    groups = filters.shape[1]
    share = chans // groups
    sub_rows = tok_rows // count_ctx
    period = 2 * count_ctx * tok_rows
    both = lax.all_to_all(
        jnp.concatenate([gated, filters], axis=1).reshape(1, tok_rows, chans + groups),
        CTX, split_axis=1, concat_axis=0, tiled=True,
    )
    got_source = both[:, :, :chans]
    got_filter = both[:, :, chans:]
    coarse_idx = jnp.arange(count_ctx, dtype=jnp.int32)
    coarse_freq = jnp.arange(2 * count_ctx, dtype=jnp.int32)
    coarse_angle = angle_table(coarse_freq, coarse_idx, 2 * count_ctx)
    cos_coarse = jnp.cos(coarse_angle)
    sin_coarse = jnp.sin(coarse_angle)
    fine_global = my_index * sub_rows + jnp.arange(sub_rows, dtype=jnp.int32)
    twist_in = angle_table(coarse_freq, fine_global, period)
    source_re, source_im = section_coarse(
        got_source.astype(jnp.float32), cos_coarse, sin_coarse, twist_in
    )
    filter_re, filter_im = section_coarse(
        got_filter.astype(jnp.float32), cos_coarse, sin_coarse, twist_in
    )
    packed = lax.all_to_all(
        jnp.concatenate([source_re, source_im, filter_re, filter_im], axis=2).astype(jnp.bfloat16),
        CTX, split_axis=0, concat_axis=1, tiled=True,
    ).astype(jnp.float32)
    source_re = packed[:, :, :chans]
    source_im = packed[:, :, chans:2 * chans]
    filter_re = packed[:, :, 2 * chans:2 * chans + groups]
    filter_im = packed[:, :, 2 * chans + groups:]
    fine_idx = jnp.arange(tok_rows, dtype=jnp.int32)
    fine_angle = angle_table(fine_idx, fine_idx, tok_rows)
    cos_fine = jnp.cos(fine_angle)
    sin_fine = jnp.sin(fine_angle)
    source_re, source_im = section_fine(source_re, source_im, cos_fine, sin_fine, -1.0)
    filter_re, filter_im = section_fine(filter_re, filter_im, cos_fine, sin_fine, -1.0)
    split_re = source_re.reshape(2, tok_rows, groups, share)
    split_im = source_im.reshape(2, tok_rows, groups, share)
    prod_re = split_re * filter_re[..., None] - split_im * filter_im[..., None]
    prod_im = split_re * filter_im[..., None] + split_im * filter_re[..., None]
    back_re, back_im = section_fine(
        prod_re.reshape(2, tok_rows, chans),
        prod_im.reshape(2, tok_rows, chans),
        cos_fine,
        sin_fine,
        1.0,
    )
    pair_freq = my_index * 2 + jnp.arange(2, dtype=jnp.int32)
    twist_out = angle_table(pair_freq, fine_idx, period)
    cos_out = jnp.cos(twist_out)[:, :, None]
    sin_out = jnp.sin(twist_out)[:, :, None]
    turned_re = back_re * cos_out - back_im * sin_out
    turned_im = back_re * sin_out + back_im * cos_out
    turned = lax.all_to_all(
        jnp.concatenate([turned_re, turned_im], axis=2).astype(jnp.bfloat16),
        CTX, split_axis=1, concat_axis=0, tiled=True,
    ).astype(jnp.float32)
    turned_re = turned[:, :, :chans]
    turned_im = turned[:, :, chans:]
    result = jnp.einsum("nk,ksc->nsc", cos_coarse.T, turned_re, precision=highest)
    result = result - jnp.einsum("nk,ksc->nsc", sin_coarse.T, turned_im, precision=highest)
    rounded = (result / period).astype(jnp.bfloat16)
    returned = lax.all_to_all(rounded, CTX, split_axis=0, concat_axis=1, tiled=True)
    return returned.reshape(tok_rows, chans)


CTX = ("z", "yh", "x")
EXP2_SCALE = math.log2(math.e) * HD ** (-0.5)
HALF = ("yh", "x")


def flash_kernel(info_ref, q_ref, k_ref, v_ref, acc_ref, m_ref, l_ref, *, heads, tok_rows, key_block, scale):
    j = pl.program_id(0)
    q_first = info_ref[0]
    last_block = info_ref[1] - 1
    key_first = j * key_block

    @pl.when(j == 0)
    def _():
        m_ref[...] = jnp.full_like(m_ref, neg_large)
        l_ref[...] = jnp.zeros_like(l_ref)
        acc_ref[...] = jnp.zeros_like(acc_ref)

    def step(masked):
        if masked:
            query_pos = q_first + lax.broadcasted_iota(jnp.int32, (tok_rows, key_block), 0)
            key_pos = key_first + lax.broadcasted_iota(jnp.int32, (tok_rows, key_block), 1)
            allowed = key_pos <= query_pos
        for h in range(heads):
            cols = slice(h * HD, (h + 1) * HD)
            scores = lax.dot_general(
                q_ref[:, cols], k_ref[:, cols], (((1,), (1,)), ((), ())),
                preferred_element_type=jnp.float32,
            )
            if masked:
                scores = jnp.where(allowed, scores, neg_large)
            m_prev = m_ref[h]
            m_new = jnp.maximum(m_prev, jnp.max(scores, axis=1, keepdims=True))
            weights = jnp.exp2((scores - m_new) * scale)
            if masked:
                weights = jnp.where(allowed, weights, 0.0)
            factor = jnp.exp2((m_prev - m_new) * scale)
            l_ref[h] = l_ref[h] * factor + jnp.sum(weights, axis=1, keepdims=True)
            acc_ref[:, cols] = acc_ref[:, cols] * factor + jnp.dot(
                weights.astype(jnp.bfloat16), v_ref[:, cols], preferred_element_type=jnp.float32
            )
            m_ref[h] = m_new

    full = key_first + key_block <= q_first

    @pl.when(jnp.logical_and(j <= last_block, full))
    def _():
        step(False)

    @pl.when(jnp.logical_and(j <= last_block, jnp.logical_not(full)))
    def _():
        step(True)


def flash_partial(queries, keys, values, q_first, needed, key_block):
    tok_rows, width = queries.shape
    heads = width // HD
    total_rows = keys.shape[0]
    info = jnp.stack([q_first, needed]).astype(jnp.int32)
    kernel = partial(flash_kernel, heads=heads, tok_rows=tok_rows, key_block=key_block, scale=EXP2_SCALE)
    kv_spec = pl.BlockSpec((key_block, width), lambda j, info: (jnp.minimum(j, info[1] - 1), 0))
    stat_spec = pl.BlockSpec((heads, tok_rows, 1), lambda j, info: (0, 0, 0))
    return pl.pallas_call(
        kernel,
        out_shape=(
            jax.ShapeDtypeStruct((tok_rows, width), jnp.float32),
            jax.ShapeDtypeStruct((heads, tok_rows, 1), jnp.float32),
            jax.ShapeDtypeStruct((heads, tok_rows, 1), jnp.float32),
        ),
        grid_spec=pltpu.PrefetchScalarGridSpec(
            num_scalar_prefetch=1,
            grid=(total_rows // key_block,),
            in_specs=[pl.BlockSpec((tok_rows, width), lambda j, info: (0, 0)), kv_spec, kv_spec],
            out_specs=[pl.BlockSpec((tok_rows, width), lambda j, info: (0, 0)), stat_spec, stat_spec],
        ),
        compiler_params=pltpu.CompilerParams(
            dimension_semantics=("arbitrary",), vmem_limit_bytes=48 * 1024 * 1024
        ),
        cost_estimate=pl.CostEstimate(
            flops=4 * tok_rows * total_rows * width,
            transcendentals=heads * tok_rows * total_rows,
            bytes_accessed=2 * total_rows * width * 2 + tok_rows * width * 6,
        ),
    )(info, queries, keys, values)


def attention(q_attn, k_attn, v_attn, tok_rows):
    width = q_attn.shape[1]
    heads = width // HD
    quarters = lax.axis_size("z")
    quarter = lax.axis_index("z")
    half_count = 1
    for name in HALF:
        half_count = half_count * lax.axis_size(name)
    my_index = lax.axis_index(CTX)
    local_index = my_index - quarter * half_count
    key_part = lax.all_gather(k_attn, HALF, axis=0, tiled=True)
    value_part = lax.all_gather(v_attn, HALF, axis=0, tiled=True)
    part_rows = key_part.shape[0]
    key_block = 896 if part_rows % 896 == 0 else tok_rows
    states = []
    for shift in range(1, quarters):
        visiting = lax.ppermute(q_attn, "z", [(k, k - shift) for k in range(shift, quarters)])
        cross = flash_partial(
            visiting, key_part, value_part, jnp.int32(part_rows), jnp.int32(part_rows // key_block), key_block
        )
        stats = jnp.concatenate([cross[1].reshape(heads, tok_rows), cross[2].reshape(heads, tok_rows)])
        back = lax.ppermute(
            jnp.concatenate([cross[0], stats.T], axis=1), "z", [(k - shift, k) for k in range(shift, quarters)]
        )
        back_stats = back[:, width:].T
        back_max = jnp.where(quarter >= shift, back_stats[:heads], neg_large)
        states.append((back[:, :width], back_max, back_stats[heads:]))
    needed = ((local_index + 1) * tok_rows + key_block - 1) // key_block
    own_acc, own_max, own_total = flash_partial(
        q_attn, key_part, value_part, local_index * tok_rows, needed, key_block
    )
    states.append((own_acc, own_max.reshape(heads, tok_rows), own_total.reshape(heads, tok_rows)))
    top = states[0][1]
    for state in states[1:]:
        top = jnp.maximum(top, state[1])
    merged = None
    totals = None
    for acc, row_max, row_total in states:
        scale = jnp.exp2((row_max - top) * EXP2_SCALE)
        part = acc.reshape(tok_rows, heads, HD) * scale.T[:, :, None]
        merged = part if merged is None else merged + part
        totals = scale * row_total if totals is None else totals + scale * row_total
    merged = merged / totals.T[:, :, None]
    return merged.reshape(tok_rows, width).astype(jnp.bfloat16)


def local(q_conv, k_conv, v_conv, conv_filter, q_attn, k_attn, v_attn, w_conv_out, w_attn_out):
    count_ctx = lax.axis_size(CTX)
    my_index = lax.axis_index(CTX)
    tok_rows = q_conv.shape[0]
    gated = (k_conv.astype(jnp.float32) * v_conv.astype(jnp.float32)).astype(jnp.bfloat16)
    conv = spectral_conv(gated, conv_filter, my_index, tok_rows, count_ctx)
    mixed = (q_conv.astype(jnp.float32) * conv.astype(jnp.float32)).astype(jnp.bfloat16)
    conv_part = jnp.dot(mixed, w_conv_out, preferred_element_type=jnp.float32)
    attended = attention(q_attn, k_attn, v_attn, tok_rows)
    return lax.psum_scatter(
        (conv_part + jnp.dot(attended, w_attn_out, preferred_element_type=jnp.float32)).astype(jnp.bfloat16),
        "ch",
        scatter_dimension=0,
        tiled=True,
    )


def solution(mesh):
    ctx_size, ch_size = mesh.devices.shape
    split_mesh = jax.sharding.Mesh(
        mesh.devices.reshape(ctx_size // 8, 2, 4, ch_size), CTX + ("ch",)
    )
    tokens = P(CTX, "ch")
    return jax.shard_map(
        local,
        mesh=split_mesh,
        in_specs=(tokens,) * 7 + (P("ch", None), P("ch", None)),
        out_specs=P(CTX + ("ch",), None),
        check_vma=False,
    )
```

```python
from functools import partial
import math

import jax
import jax.numpy as jnp
from jax import lax
from jax.sharding import PartitionSpec as P
from jax.experimental import pallas as pl
from jax.experimental.pallas import tpu as pltpu

HD = 128


two_pi = 2.0 * math.pi
neg_large = -1e30
highest = lax.Precision.HIGHEST


def angle_table(left_idx, right_idx, period):
    product = left_idx[:, None] * right_idx[None, :] % period
    return product.astype(jnp.float32) * (two_pi / period)


def section_coarse(values, cos_table, sin_table, twiddle):
    real_part = jnp.einsum("kn,nsc->ksc", cos_table, values, precision=highest)
    imag_part = -jnp.einsum("kn,nsc->ksc", sin_table, values, precision=highest)
    cos_twist = jnp.cos(twiddle)[:, :, None]
    sin_twist = jnp.sin(twiddle)[:, :, None]
    return (
        real_part * cos_twist + imag_part * sin_twist,
        imag_part * cos_twist - real_part * sin_twist,
    )


def section_fine(real_part, imag_part, cos_table, sin_table, direction):
    cos_real = jnp.einsum("kn,anc->akc", cos_table, real_part, precision=highest)
    cos_imag = jnp.einsum("kn,anc->akc", cos_table, imag_part, precision=highest)
    sin_real = jnp.einsum("kn,anc->akc", sin_table, real_part, precision=highest)
    sin_imag = jnp.einsum("kn,anc->akc", sin_table, imag_part, precision=highest)
    return (cos_real - direction * sin_imag, cos_imag + direction * sin_real)


def spectral_conv(gated, filters, my_index, tok_rows, count_ctx):
    chans = gated.shape[1]
    groups = filters.shape[1]
    share = chans // groups
    sub_rows = tok_rows // count_ctx
    period = 2 * count_ctx * tok_rows
    both = lax.all_to_all(
        jnp.concatenate([gated, filters], axis=1).reshape(1, tok_rows, chans + groups),
        CTX, split_axis=1, concat_axis=0, tiled=True,
    )
    got_source = both[:, :, :chans]
    got_filter = both[:, :, chans:]
    coarse_idx = jnp.arange(count_ctx, dtype=jnp.int32)
    coarse_freq = jnp.arange(2 * count_ctx, dtype=jnp.int32)
    coarse_angle = angle_table(coarse_freq, coarse_idx, 2 * count_ctx)
    cos_coarse = jnp.cos(coarse_angle)
    sin_coarse = jnp.sin(coarse_angle)
    fine_global = my_index * sub_rows + jnp.arange(sub_rows, dtype=jnp.int32)
    twist_in = angle_table(coarse_freq, fine_global, period)
    source_re, source_im = section_coarse(
        got_source.astype(jnp.float32), cos_coarse, sin_coarse, twist_in
    )
    filter_re, filter_im = section_coarse(
        got_filter.astype(jnp.float32), cos_coarse, sin_coarse, twist_in
    )
    packed = lax.all_to_all(
        jnp.concatenate([source_re, source_im, filter_re, filter_im], axis=2).astype(jnp.bfloat16),
        CTX, split_axis=0, concat_axis=1, tiled=True,
    ).astype(jnp.float32)
    source_re = packed[:, :, :chans]
    source_im = packed[:, :, chans:2 * chans]
    filter_re = packed[:, :, 2 * chans:2 * chans + groups]
    filter_im = packed[:, :, 2 * chans + groups:]
    fine_idx = jnp.arange(tok_rows, dtype=jnp.int32)
    fine_angle = angle_table(fine_idx, fine_idx, tok_rows)
    cos_fine = jnp.cos(fine_angle)
    sin_fine = jnp.sin(fine_angle)
    source_re, source_im = section_fine(source_re, source_im, cos_fine, sin_fine, -1.0)
    filter_re, filter_im = section_fine(filter_re, filter_im, cos_fine, sin_fine, -1.0)
    split_re = source_re.reshape(2, tok_rows, groups, share)
    split_im = source_im.reshape(2, tok_rows, groups, share)
    prod_re = split_re * filter_re[..., None] - split_im * filter_im[..., None]
    prod_im = split_re * filter_im[..., None] + split_im * filter_re[..., None]
    back_re, back_im = section_fine(
        prod_re.reshape(2, tok_rows, chans),
        prod_im.reshape(2, tok_rows, chans),
        cos_fine,
        sin_fine,
        1.0,
    )
    pair_freq = my_index * 2 + jnp.arange(2, dtype=jnp.int32)
    twist_out = angle_table(pair_freq, fine_idx, period)
    cos_out = jnp.cos(twist_out)[:, :, None]
    sin_out = jnp.sin(twist_out)[:, :, None]
    turned_re = back_re * cos_out - back_im * sin_out
    turned_im = back_re * sin_out + back_im * cos_out
    turned = lax.all_to_all(
        jnp.concatenate([turned_re, turned_im], axis=2).astype(jnp.bfloat16),
        CTX, split_axis=1, concat_axis=0, tiled=True,
    ).astype(jnp.float32)
    turned_re = turned[:, :, :chans]
    turned_im = turned[:, :, chans:]
    result = jnp.einsum("nk,ksc->nsc", cos_coarse.T, turned_re, precision=highest)
    result = result - jnp.einsum("nk,ksc->nsc", sin_coarse.T, turned_im, precision=highest)
    rounded = (result / period).astype(jnp.bfloat16)
    returned = lax.all_to_all(rounded, CTX, split_axis=0, concat_axis=1, tiled=True)
    return returned.reshape(tok_rows, chans)


CTX = ("z", "yh", "x")
EXP2_SCALE = math.log2(math.e) * HD ** (-0.5)
HALF = ("yh", "x")


def flash_kernel(info_ref, q_ref, k_ref, v_ref, acc_ref, m_ref, l_ref, *, heads, tok_rows, key_block, scale):
    j = pl.program_id(0)
    q_first = info_ref[0]
    last_block = info_ref[1] - 1
    key_first = j * key_block

    @pl.when(j == 0)
    def _():
        m_ref[...] = jnp.full_like(m_ref, neg_large)
        l_ref[...] = jnp.zeros_like(l_ref)
        acc_ref[...] = jnp.zeros_like(acc_ref)

    def step(masked):
        if masked:
            query_pos = q_first + lax.broadcasted_iota(jnp.int32, (tok_rows, key_block), 0)
            key_pos = key_first + lax.broadcasted_iota(jnp.int32, (tok_rows, key_block), 1)
            allowed = key_pos <= query_pos
        def one_head(h, carry):
            cols = pl.ds(pl.multiple_of(h * HD, HD), HD)
            scores = lax.dot_general(
                q_ref[:, cols], k_ref[:, cols], (((1,), (1,)), ((), ())),
                preferred_element_type=jnp.float32,
            )
            if masked:
                scores = jnp.where(allowed, scores, neg_large)
            m_prev = m_ref[h]
            m_new = jnp.maximum(m_prev, jnp.max(scores, axis=1, keepdims=True))
            weights = jnp.exp2((scores - m_new) * scale)
            if masked:
                weights = jnp.where(allowed, weights, 0.0)
            factor = jnp.exp2((m_prev - m_new) * scale)
            l_ref[h] = l_ref[h] * factor + jnp.sum(weights, axis=1, keepdims=True)
            acc_ref[:, cols] = acc_ref[:, cols] * factor + jnp.dot(
                weights.astype(jnp.bfloat16), v_ref[:, cols], preferred_element_type=jnp.float32
            )
            m_ref[h] = m_new
            return carry

        lax.fori_loop(0, heads, one_head, 0)

    full = key_first + key_block <= q_first

    @pl.when(jnp.logical_and(j <= last_block, full))
    def _():
        step(False)

    @pl.when(jnp.logical_and(j <= last_block, jnp.logical_not(full)))
    def _():
        step(True)


def flash_partial(queries, keys, values, q_first, needed, key_block):
    tok_rows, width = queries.shape
    heads = width // HD
    total_rows = keys.shape[0]
    info = jnp.stack([q_first, needed]).astype(jnp.int32)
    kernel = partial(flash_kernel, heads=heads, tok_rows=tok_rows, key_block=key_block, scale=EXP2_SCALE)
    kv_spec = pl.BlockSpec((key_block, width), lambda j, info: (jnp.minimum(j, info[1] - 1), 0))
    stat_spec = pl.BlockSpec((heads, tok_rows, 1), lambda j, info: (0, 0, 0))
    return pl.pallas_call(
        kernel,
        out_shape=(
            jax.ShapeDtypeStruct((tok_rows, width), jnp.float32),
            jax.ShapeDtypeStruct((heads, tok_rows, 1), jnp.float32),
            jax.ShapeDtypeStruct((heads, tok_rows, 1), jnp.float32),
        ),
        grid_spec=pltpu.PrefetchScalarGridSpec(
            num_scalar_prefetch=1,
            grid=(total_rows // key_block,),
            in_specs=[pl.BlockSpec((tok_rows, width), lambda j, info: (0, 0)), kv_spec, kv_spec],
            out_specs=[pl.BlockSpec((tok_rows, width), lambda j, info: (0, 0)), stat_spec, stat_spec],
        ),
        compiler_params=pltpu.CompilerParams(
            dimension_semantics=("arbitrary",), vmem_limit_bytes=48 * 1024 * 1024
        ),
        cost_estimate=pl.CostEstimate(
            flops=4 * tok_rows * total_rows * width,
            transcendentals=heads * tok_rows * total_rows,
            bytes_accessed=2 * total_rows * width * 2 + tok_rows * width * 6,
        ),
    )(info, queries, keys, values)


def attention(q_attn, k_attn, v_attn, tok_rows):
    width = q_attn.shape[1]
    heads = width // HD
    quarters = lax.axis_size("z")
    quarter = lax.axis_index("z")
    half_count = 1
    for name in HALF:
        half_count = half_count * lax.axis_size(name)
    my_index = lax.axis_index(CTX)
    local_index = my_index - quarter * half_count
    key_part = lax.all_gather(k_attn, HALF, axis=0, tiled=True)
    value_part = lax.all_gather(v_attn, HALF, axis=0, tiled=True)
    part_rows = key_part.shape[0]
    key_block = 896 if part_rows % 896 == 0 else tok_rows
    states = []
    for shift in range(1, quarters):
        visiting = lax.ppermute(q_attn, "z", [(k, k - shift) for k in range(shift, quarters)])
        cross = flash_partial(
            visiting, key_part, value_part, jnp.int32(part_rows), jnp.int32(part_rows // key_block), key_block
        )
        stats = jnp.concatenate([cross[1].reshape(heads, tok_rows), cross[2].reshape(heads, tok_rows)])
        back = lax.ppermute(
            jnp.concatenate([cross[0], stats.T], axis=1), "z", [(k - shift, k) for k in range(shift, quarters)]
        )
        back_stats = back[:, width:].T
        back_max = jnp.where(quarter >= shift, back_stats[:heads], neg_large)
        states.append((back[:, :width], back_max, back_stats[heads:]))
    needed = ((local_index + 1) * tok_rows + key_block - 1) // key_block
    own_acc, own_max, own_total = flash_partial(
        q_attn, key_part, value_part, local_index * tok_rows, needed, key_block
    )
    states.append((own_acc, own_max.reshape(heads, tok_rows), own_total.reshape(heads, tok_rows)))
    top = states[0][1]
    for state in states[1:]:
        top = jnp.maximum(top, state[1])
    merged = None
    totals = None
    for acc, row_max, row_total in states:
        scale = jnp.exp2((row_max - top) * EXP2_SCALE)
        part = acc.reshape(tok_rows, heads, HD) * scale.T[:, :, None]
        merged = part if merged is None else merged + part
        totals = scale * row_total if totals is None else totals + scale * row_total
    merged = merged / totals.T[:, :, None]
    return merged.reshape(tok_rows, width).astype(jnp.bfloat16)


def local(q_conv, k_conv, v_conv, conv_filter, q_attn, k_attn, v_attn, w_conv_out, w_attn_out):
    count_ctx = lax.axis_size(CTX)
    my_index = lax.axis_index(CTX)
    tok_rows = q_conv.shape[0]
    gated = (k_conv.astype(jnp.float32) * v_conv.astype(jnp.float32)).astype(jnp.bfloat16)
    conv = spectral_conv(gated, conv_filter, my_index, tok_rows, count_ctx)
    mixed = (q_conv.astype(jnp.float32) * conv.astype(jnp.float32)).astype(jnp.bfloat16)
    conv_part = jnp.dot(mixed, w_conv_out, preferred_element_type=jnp.float32)
    attended = attention(q_attn, k_attn, v_attn, tok_rows)
    return lax.psum_scatter(
        (conv_part + jnp.dot(attended, w_attn_out, preferred_element_type=jnp.float32)).astype(jnp.bfloat16),
        "ch",
        scatter_dimension=0,
        tiled=True,
    )


def solution(mesh):
    ctx_size, ch_size = mesh.devices.shape
    split_mesh = jax.sharding.Mesh(
        mesh.devices.reshape(ctx_size // 8, 2, 4, ch_size), CTX + ("ch",)
    )
    tokens = P(CTX, "ch")
    return jax.shard_map(
        local,
        mesh=split_mesh,
        in_specs=(tokens,) * 7 + (P("ch", None), P("ch", None)),
        out_specs=P(CTX + ("ch",), None),
        check_vma=False,
    )
```

```python
from functools import partial
import math

import jax
import jax.numpy as jnp
from jax import lax
from jax.sharding import PartitionSpec as P
from jax.experimental import pallas as pl
from jax.experimental.pallas import tpu as pltpu

HD = 128


two_pi = 2.0 * math.pi
neg_large = -1e30
highest = lax.Precision.HIGHEST


def angle_table(left_idx, right_idx, period):
    product = left_idx[:, None] * right_idx[None, :] % period
    return product.astype(jnp.float32) * (two_pi / period)


def section_coarse(values, cos_table, sin_table, twiddle):
    real_part = jnp.einsum("kn,nsc->ksc", cos_table, values, precision=highest)
    imag_part = -jnp.einsum("kn,nsc->ksc", sin_table, values, precision=highest)
    cos_twist = jnp.cos(twiddle)[:, :, None]
    sin_twist = jnp.sin(twiddle)[:, :, None]
    return (
        real_part * cos_twist + imag_part * sin_twist,
        imag_part * cos_twist - real_part * sin_twist,
    )


def section_fine(real_part, imag_part, cos_table, sin_table, direction):
    cos_real = jnp.einsum("kn,anc->akc", cos_table, real_part, precision=highest)
    cos_imag = jnp.einsum("kn,anc->akc", cos_table, imag_part, precision=highest)
    sin_real = jnp.einsum("kn,anc->akc", sin_table, real_part, precision=highest)
    sin_imag = jnp.einsum("kn,anc->akc", sin_table, imag_part, precision=highest)
    return (cos_real - direction * sin_imag, cos_imag + direction * sin_real)


def spectral_conv(gated, filters, my_index, tok_rows, count_ctx):
    chans = gated.shape[1]
    groups = filters.shape[1]
    share = chans // groups
    sub_rows = tok_rows // count_ctx
    period = 2 * count_ctx * tok_rows
    both = lax.all_to_all(
        jnp.concatenate([gated, filters], axis=1).reshape(1, tok_rows, chans + groups),
        CTX, split_axis=1, concat_axis=0, tiled=True,
    )
    got_source = both[:, :, :chans]
    got_filter = both[:, :, chans:]
    coarse_idx = jnp.arange(count_ctx, dtype=jnp.int32)
    coarse_freq = jnp.arange(2 * count_ctx, dtype=jnp.int32)
    coarse_angle = angle_table(coarse_freq, coarse_idx, 2 * count_ctx)
    cos_coarse = jnp.cos(coarse_angle)
    sin_coarse = jnp.sin(coarse_angle)
    fine_global = my_index * sub_rows + jnp.arange(sub_rows, dtype=jnp.int32)
    twist_in = angle_table(coarse_freq, fine_global, period)
    source_re, source_im = section_coarse(
        got_source.astype(jnp.float32), cos_coarse, sin_coarse, twist_in
    )
    filter_re, filter_im = section_coarse(
        got_filter.astype(jnp.float32), cos_coarse, sin_coarse, twist_in
    )
    packed = lax.all_to_all(
        jnp.concatenate([source_re, source_im, filter_re, filter_im], axis=2).astype(jnp.bfloat16),
        CTX, split_axis=0, concat_axis=1, tiled=True,
    ).astype(jnp.float32)
    source_re = packed[:, :, :chans]
    source_im = packed[:, :, chans:2 * chans]
    filter_re = packed[:, :, 2 * chans:2 * chans + groups]
    filter_im = packed[:, :, 2 * chans + groups:]
    fine_idx = jnp.arange(tok_rows, dtype=jnp.int32)
    fine_angle = angle_table(fine_idx, fine_idx, tok_rows)
    cos_fine = jnp.cos(fine_angle)
    sin_fine = jnp.sin(fine_angle)
    source_re, source_im = section_fine(source_re, source_im, cos_fine, sin_fine, -1.0)
    filter_re, filter_im = section_fine(filter_re, filter_im, cos_fine, sin_fine, -1.0)
    split_re = source_re.reshape(2, tok_rows, groups, share)
    split_im = source_im.reshape(2, tok_rows, groups, share)
    prod_re = split_re * filter_re[..., None] - split_im * filter_im[..., None]
    prod_im = split_re * filter_im[..., None] + split_im * filter_re[..., None]
    back_re, back_im = section_fine(
        prod_re.reshape(2, tok_rows, chans),
        prod_im.reshape(2, tok_rows, chans),
        cos_fine,
        sin_fine,
        1.0,
    )
    pair_freq = my_index * 2 + jnp.arange(2, dtype=jnp.int32)
    twist_out = angle_table(pair_freq, fine_idx, period)
    cos_out = jnp.cos(twist_out)[:, :, None]
    sin_out = jnp.sin(twist_out)[:, :, None]
    turned_re = back_re * cos_out - back_im * sin_out
    turned_im = back_re * sin_out + back_im * cos_out
    turned = lax.all_to_all(
        jnp.concatenate([turned_re, turned_im], axis=2).astype(jnp.bfloat16),
        CTX, split_axis=1, concat_axis=0, tiled=True,
    ).astype(jnp.float32)
    turned_re = turned[:, :, :chans]
    turned_im = turned[:, :, chans:]
    result = jnp.einsum("nk,ksc->nsc", cos_coarse.T, turned_re, precision=highest)
    result = result - jnp.einsum("nk,ksc->nsc", sin_coarse.T, turned_im, precision=highest)
    rounded = (result / period).astype(jnp.bfloat16)
    returned = lax.all_to_all(rounded, CTX, split_axis=0, concat_axis=1, tiled=True)
    return returned.reshape(tok_rows, chans)


CTX = ("z", "yh", "x")
GROUP = ("z", "yh")
EXP2_SCALE = math.log2(math.e) * HD ** (-0.5)
HALF = ("x",)


def flash_kernel(info_ref, q_ref, k_ref, v_ref, acc_ref, m_ref, l_ref, *, heads, tok_rows, key_block, scale):
    j = pl.program_id(0)
    q_first = info_ref[0]
    last_block = info_ref[1] - 1
    key_first = j * key_block

    @pl.when(j == 0)
    def _():
        m_ref[...] = jnp.full_like(m_ref, neg_large)
        l_ref[...] = jnp.zeros_like(l_ref)
        acc_ref[...] = jnp.zeros_like(acc_ref)

    def step(masked):
        if masked:
            query_pos = q_first + lax.broadcasted_iota(jnp.int32, (tok_rows, key_block), 0)
            key_pos = key_first + lax.broadcasted_iota(jnp.int32, (tok_rows, key_block), 1)
            allowed = key_pos <= query_pos
        for h in range(heads):
            cols = slice(h * HD, (h + 1) * HD)
            scores = lax.dot_general(
                q_ref[:, cols], k_ref[:, cols], (((1,), (1,)), ((), ())),
                preferred_element_type=jnp.float32,
            )
            if masked:
                scores = jnp.where(allowed, scores, neg_large)
            m_prev = m_ref[h]
            m_new = jnp.maximum(m_prev, jnp.max(scores, axis=1, keepdims=True))
            weights = jnp.exp2((scores - m_new) * scale)
            if masked:
                weights = jnp.where(allowed, weights, 0.0)
            factor = jnp.exp2((m_prev - m_new) * scale)
            l_ref[h] = l_ref[h] * factor + jnp.sum(weights, axis=1, keepdims=True)
            acc_ref[:, cols] = acc_ref[:, cols] * factor + jnp.dot(
                weights.astype(jnp.bfloat16), v_ref[:, cols], preferred_element_type=jnp.float32
            )
            m_ref[h] = m_new

    full = key_first + key_block <= q_first

    @pl.when(jnp.logical_and(j <= last_block, full))
    def _():
        step(False)

    @pl.when(jnp.logical_and(j <= last_block, jnp.logical_not(full)))
    def _():
        step(True)


def flash_partial(queries, keys, values, q_first, needed, key_block):
    tok_rows, width = queries.shape
    heads = width // HD
    total_rows = keys.shape[0]
    info = jnp.stack([q_first, needed]).astype(jnp.int32)
    kernel = partial(flash_kernel, heads=heads, tok_rows=tok_rows, key_block=key_block, scale=EXP2_SCALE)
    kv_spec = pl.BlockSpec((key_block, width), lambda j, info: (jnp.minimum(j, info[1] - 1), 0))
    stat_spec = pl.BlockSpec((heads, tok_rows, 1), lambda j, info: (0, 0, 0))
    return pl.pallas_call(
        kernel,
        out_shape=(
            jax.ShapeDtypeStruct((tok_rows, width), jnp.float32),
            jax.ShapeDtypeStruct((heads, tok_rows, 1), jnp.float32),
            jax.ShapeDtypeStruct((heads, tok_rows, 1), jnp.float32),
        ),
        grid_spec=pltpu.PrefetchScalarGridSpec(
            num_scalar_prefetch=1,
            grid=(total_rows // key_block,),
            in_specs=[pl.BlockSpec((tok_rows, width), lambda j, info: (0, 0)), kv_spec, kv_spec],
            out_specs=[pl.BlockSpec((tok_rows, width), lambda j, info: (0, 0)), stat_spec, stat_spec],
        ),
        compiler_params=pltpu.CompilerParams(
            dimension_semantics=("arbitrary",), vmem_limit_bytes=48 * 1024 * 1024
        ),
        cost_estimate=pl.CostEstimate(
            flops=4 * tok_rows * total_rows * width,
            transcendentals=heads * tok_rows * total_rows,
            bytes_accessed=2 * total_rows * width * 2 + tok_rows * width * 6,
        ),
    )(info, queries, keys, values)


def attention(q_attn, k_attn, v_attn, tok_rows):
    width = q_attn.shape[1]
    heads = width // HD
    quarters = 1
    for name in GROUP:
        quarters = quarters * lax.axis_size(name)
    quarter = lax.axis_index(GROUP)
    half_count = 1
    for name in HALF:
        half_count = half_count * lax.axis_size(name)
    my_index = lax.axis_index(CTX)
    local_index = my_index - quarter * half_count
    key_part = lax.all_gather(k_attn, HALF, axis=0, tiled=True)
    value_part = lax.all_gather(v_attn, HALF, axis=0, tiled=True)
    part_rows = key_part.shape[0]
    key_block = 896 if part_rows % 896 == 0 else tok_rows
    states = []
    for shift in range(1, quarters):
        visiting = lax.ppermute(q_attn, GROUP, [(k, k - shift) for k in range(shift, quarters)])
        cross = flash_partial(
            visiting, key_part, value_part, jnp.int32(part_rows), jnp.int32(part_rows // key_block), key_block
        )
        stats = jnp.concatenate([cross[1].reshape(heads, tok_rows), cross[2].reshape(heads, tok_rows)])
        back = lax.ppermute(
            jnp.concatenate([cross[0], stats.T], axis=1), GROUP, [(k - shift, k) for k in range(shift, quarters)]
        )
        back_stats = back[:, width:].T
        back_max = jnp.where(quarter >= shift, back_stats[:heads], neg_large)
        states.append((back[:, :width], back_max, back_stats[heads:]))
    needed = ((local_index + 1) * tok_rows + key_block - 1) // key_block
    own_acc, own_max, own_total = flash_partial(
        q_attn, key_part, value_part, local_index * tok_rows, needed, key_block
    )
    states.append((own_acc, own_max.reshape(heads, tok_rows), own_total.reshape(heads, tok_rows)))
    top = states[0][1]
    for state in states[1:]:
        top = jnp.maximum(top, state[1])
    merged = None
    totals = None
    for acc, row_max, row_total in states:
        scale = jnp.exp2((row_max - top) * EXP2_SCALE)
        part = acc.reshape(tok_rows, heads, HD) * scale.T[:, :, None]
        merged = part if merged is None else merged + part
        totals = scale * row_total if totals is None else totals + scale * row_total
    merged = merged / totals.T[:, :, None]
    return merged.reshape(tok_rows, width).astype(jnp.bfloat16)


def local(q_conv, k_conv, v_conv, conv_filter, q_attn, k_attn, v_attn, w_conv_out, w_attn_out):
    count_ctx = lax.axis_size(CTX)
    my_index = lax.axis_index(CTX)
    tok_rows = q_conv.shape[0]
    gated = (k_conv.astype(jnp.float32) * v_conv.astype(jnp.float32)).astype(jnp.bfloat16)
    conv = spectral_conv(gated, conv_filter, my_index, tok_rows, count_ctx)
    mixed = (q_conv.astype(jnp.float32) * conv.astype(jnp.float32)).astype(jnp.bfloat16)
    conv_part = jnp.dot(mixed, w_conv_out, preferred_element_type=jnp.float32)
    attended = attention(q_attn, k_attn, v_attn, tok_rows)
    return lax.psum_scatter(
        (conv_part + jnp.dot(attended, w_attn_out, preferred_element_type=jnp.float32)).astype(jnp.bfloat16),
        "ch",
        scatter_dimension=0,
        tiled=True,
    )


def solution(mesh):
    ctx_size, ch_size = mesh.devices.shape
    split_mesh = jax.sharding.Mesh(
        mesh.devices.reshape(ctx_size // 8, 2, 4, ch_size), CTX + ("ch",)
    )
    tokens = P(CTX, "ch")
    return jax.shard_map(
        local,
        mesh=split_mesh,
        in_specs=(tokens,) * 7 + (P("ch", None), P("ch", None)),
        out_specs=P(CTX + ("ch",), None),
        check_vma=False,
    )
```

```python
from functools import partial
import math

import jax
import jax.numpy as jnp
from jax import lax
from jax.sharding import PartitionSpec as P
from jax.experimental import pallas as pl
from jax.experimental.pallas import tpu as pltpu

HD = 128


two_pi = 2.0 * math.pi
neg_large = -1e30
highest = lax.Precision.HIGHEST


def angle_table(left_idx, right_idx, period):
    product = left_idx[:, None] * right_idx[None, :] % period
    return product.astype(jnp.float32) * (two_pi / period)


def section_coarse(values, cos_table, sin_table, twiddle):
    real_part = jnp.einsum("kn,nsc->ksc", cos_table, values, precision=highest)
    imag_part = -jnp.einsum("kn,nsc->ksc", sin_table, values, precision=highest)
    cos_twist = jnp.cos(twiddle)[:, :, None]
    sin_twist = jnp.sin(twiddle)[:, :, None]
    return (
        real_part * cos_twist + imag_part * sin_twist,
        imag_part * cos_twist - real_part * sin_twist,
    )


def section_fine(real_part, imag_part, cos_table, sin_table, direction):
    cos_real = jnp.einsum("kn,anc->akc", cos_table, real_part, precision=highest)
    cos_imag = jnp.einsum("kn,anc->akc", cos_table, imag_part, precision=highest)
    sin_real = jnp.einsum("kn,anc->akc", sin_table, real_part, precision=highest)
    sin_imag = jnp.einsum("kn,anc->akc", sin_table, imag_part, precision=highest)
    return (cos_real - direction * sin_imag, cos_imag + direction * sin_real)


def spectral_conv(gated, filters, my_index, tok_rows, count_ctx):
    chans = gated.shape[1]
    groups = filters.shape[1]
    share = chans // groups
    sub_rows = tok_rows // count_ctx
    period = 2 * count_ctx * tok_rows
    both = lax.all_to_all(
        jnp.concatenate([gated, filters], axis=1).reshape(1, tok_rows, chans + groups),
        CTX, split_axis=1, concat_axis=0, tiled=True,
    )
    got_source = both[:, :, :chans]
    got_filter = both[:, :, chans:]
    coarse_idx = jnp.arange(count_ctx, dtype=jnp.int32)
    coarse_freq = jnp.arange(2 * count_ctx, dtype=jnp.int32)
    coarse_angle = angle_table(coarse_freq, coarse_idx, 2 * count_ctx)
    cos_coarse = jnp.cos(coarse_angle)
    sin_coarse = jnp.sin(coarse_angle)
    fine_global = my_index * sub_rows + jnp.arange(sub_rows, dtype=jnp.int32)
    twist_in = angle_table(coarse_freq, fine_global, period)
    source_re, source_im = section_coarse(
        got_source.astype(jnp.float32), cos_coarse, sin_coarse, twist_in
    )
    filter_re, filter_im = section_coarse(
        got_filter.astype(jnp.float32), cos_coarse, sin_coarse, twist_in
    )
    packed = lax.all_to_all(
        jnp.concatenate([source_re, source_im, filter_re, filter_im], axis=2).astype(jnp.bfloat16),
        CTX, split_axis=0, concat_axis=1, tiled=True,
    ).astype(jnp.float32)
    source_re = packed[:, :, :chans]
    source_im = packed[:, :, chans:2 * chans]
    filter_re = packed[:, :, 2 * chans:2 * chans + groups]
    filter_im = packed[:, :, 2 * chans + groups:]
    fine_idx = jnp.arange(tok_rows, dtype=jnp.int32)
    fine_angle = angle_table(fine_idx, fine_idx, tok_rows)
    cos_fine = jnp.cos(fine_angle)
    sin_fine = jnp.sin(fine_angle)
    source_re, source_im = section_fine(source_re, source_im, cos_fine, sin_fine, -1.0)
    filter_re, filter_im = section_fine(filter_re, filter_im, cos_fine, sin_fine, -1.0)
    split_re = source_re.reshape(2, tok_rows, groups, share)
    split_im = source_im.reshape(2, tok_rows, groups, share)
    prod_re = split_re * filter_re[..., None] - split_im * filter_im[..., None]
    prod_im = split_re * filter_im[..., None] + split_im * filter_re[..., None]
    back_re, back_im = section_fine(
        prod_re.reshape(2, tok_rows, chans),
        prod_im.reshape(2, tok_rows, chans),
        cos_fine,
        sin_fine,
        1.0,
    )
    pair_freq = my_index * 2 + jnp.arange(2, dtype=jnp.int32)
    twist_out = angle_table(pair_freq, fine_idx, period)
    cos_out = jnp.cos(twist_out)[:, :, None]
    sin_out = jnp.sin(twist_out)[:, :, None]
    turned_re = back_re * cos_out - back_im * sin_out
    turned_im = back_re * sin_out + back_im * cos_out
    turned = lax.all_to_all(
        jnp.concatenate([turned_re, turned_im], axis=2).astype(jnp.bfloat16),
        CTX, split_axis=1, concat_axis=0, tiled=True,
    ).astype(jnp.float32)
    turned_re = turned[:, :, :chans]
    turned_im = turned[:, :, chans:]
    result = jnp.einsum("nk,ksc->nsc", cos_coarse.T, turned_re, precision=highest)
    result = result - jnp.einsum("nk,ksc->nsc", sin_coarse.T, turned_im, precision=highest)
    rounded = (result / period).astype(jnp.bfloat16)
    returned = lax.all_to_all(rounded, CTX, split_axis=0, concat_axis=1, tiled=True)
    return returned.reshape(tok_rows, chans)


CTX = ("z", "yh", "x")
EXP2_SCALE = math.log2(math.e) * HD ** (-0.5)
HALF = ("yh", "x")


def flash_kernel(info_ref, q_ref, k_ref, v_ref, acc_ref, m_ref, l_ref, *, heads, tok_rows, key_block, scale):
    j = pl.program_id(0)
    q_first = info_ref[0]
    last_block = info_ref[1] - 1
    key_first = j * key_block

    @pl.when(j == 0)
    def _():
        m_ref[...] = jnp.full_like(m_ref, neg_large)
        l_ref[...] = jnp.zeros_like(l_ref)
        acc_ref[...] = jnp.zeros_like(acc_ref)

    def step(masked):
        if masked:
            query_pos = q_first + lax.broadcasted_iota(jnp.int32, (tok_rows, key_block), 0)
            key_pos = key_first + lax.broadcasted_iota(jnp.int32, (tok_rows, key_block), 1)
            allowed = key_pos <= query_pos
        for h in range(heads):
            cols = slice(h * HD, (h + 1) * HD)
            scores = lax.dot_general(
                q_ref[:, cols], k_ref[:, cols], (((1,), (1,)), ((), ())),
                preferred_element_type=jnp.float32,
            )
            if masked:
                scores = jnp.where(allowed, scores, neg_large)
            m_prev = m_ref[h]
            m_new = jnp.maximum(m_prev, jnp.max(scores, axis=1, keepdims=True))
            weights = jnp.exp2((scores - m_new) * scale)
            if masked:
                weights = jnp.where(allowed, weights, 0.0)
            factor = jnp.exp2((m_prev - m_new) * scale)
            l_ref[h] = l_ref[h] * factor + jnp.sum(weights, axis=1, keepdims=True)
            acc_ref[:, cols] = acc_ref[:, cols] * factor + jnp.dot(
                weights.astype(jnp.bfloat16), v_ref[:, cols], preferred_element_type=jnp.float32
            )
            m_ref[h] = m_new

    full = key_first + key_block <= q_first

    @pl.when(jnp.logical_and(j <= last_block, full))
    def _():
        step(False)

    @pl.when(jnp.logical_and(j <= last_block, jnp.logical_not(full)))
    def _():
        step(True)


def flash_partial(queries, keys, values, q_first, needed, key_block):
    tok_rows, width = queries.shape
    heads = width // HD
    total_rows = keys.shape[0]
    info = jnp.stack([q_first, needed]).astype(jnp.int32)
    kernel = partial(flash_kernel, heads=heads, tok_rows=tok_rows, key_block=key_block, scale=EXP2_SCALE)
    kv_spec = pl.BlockSpec((key_block, width), lambda j, info: (jnp.minimum(j, info[1] - 1), 0))
    stat_spec = pl.BlockSpec((heads, tok_rows, 1), lambda j, info: (0, 0, 0))
    return pl.pallas_call(
        kernel,
        out_shape=(
            jax.ShapeDtypeStruct((tok_rows, width), jnp.float32),
            jax.ShapeDtypeStruct((heads, tok_rows, 1), jnp.float32),
            jax.ShapeDtypeStruct((heads, tok_rows, 1), jnp.float32),
        ),
        grid_spec=pltpu.PrefetchScalarGridSpec(
            num_scalar_prefetch=1,
            grid=(total_rows // key_block,),
            in_specs=[pl.BlockSpec((tok_rows, width), lambda j, info: (0, 0)), kv_spec, kv_spec],
            out_specs=[pl.BlockSpec((tok_rows, width), lambda j, info: (0, 0)), stat_spec, stat_spec],
        ),
        compiler_params=pltpu.CompilerParams(
            dimension_semantics=("arbitrary",), vmem_limit_bytes=48 * 1024 * 1024
        ),
        cost_estimate=pl.CostEstimate(
            flops=4 * tok_rows * total_rows * width,
            transcendentals=heads * tok_rows * total_rows,
            bytes_accessed=2 * total_rows * width * 2 + tok_rows * width * 6,
        ),
    )(info, queries, keys, values)


def attention(q_attn, k_attn, v_attn, tok_rows):
    width = q_attn.shape[1]
    heads = width // HD
    quarters = lax.axis_size("z")
    quarter = lax.axis_index("z")
    half_count = 1
    for name in HALF:
        half_count = half_count * lax.axis_size(name)
    my_index = lax.axis_index(CTX)
    local_index = my_index - quarter * half_count
    key_part = lax.all_gather(k_attn, HALF, axis=0, tiled=True)
    value_part = lax.all_gather(v_attn, HALF, axis=0, tiled=True)
    part_rows = key_part.shape[0]
    key_block = 896 if part_rows % 896 == 0 else tok_rows
    states = []
    shifts = list(range(1, quarters))
    visiting = jnp.concatenate(
        [lax.ppermute(q_attn, "z", [(k, k - shift) for k in range(shift, quarters)]) for shift in shifts]
    )
    cross = flash_partial(
        visiting, key_part, value_part, jnp.int32(part_rows), jnp.int32(part_rows // key_block), key_block
    )
    for slot, shift in enumerate(shifts):
        rows = slice(slot * tok_rows, (slot + 1) * tok_rows)
        stats = jnp.concatenate(
            [cross[1][:, rows].reshape(heads, tok_rows), cross[2][:, rows].reshape(heads, tok_rows)]
        )
        back = lax.ppermute(
            jnp.concatenate([cross[0][rows], stats.T], axis=1), "z", [(k - shift, k) for k in range(shift, quarters)]
        )
        back_stats = back[:, width:].T
        back_max = jnp.where(quarter >= shift, back_stats[:heads], neg_large)
        states.append((back[:, :width], back_max, back_stats[heads:]))
    needed = ((local_index + 1) * tok_rows + key_block - 1) // key_block
    own_acc, own_max, own_total = flash_partial(
        q_attn, key_part, value_part, local_index * tok_rows, needed, key_block
    )
    states.append((own_acc, own_max.reshape(heads, tok_rows), own_total.reshape(heads, tok_rows)))
    top = states[0][1]
    for state in states[1:]:
        top = jnp.maximum(top, state[1])
    merged = None
    totals = None
    for acc, row_max, row_total in states:
        scale = jnp.exp2((row_max - top) * EXP2_SCALE)
        part = acc.reshape(tok_rows, heads, HD) * scale.T[:, :, None]
        merged = part if merged is None else merged + part
        totals = scale * row_total if totals is None else totals + scale * row_total
    merged = merged / totals.T[:, :, None]
    return merged.reshape(tok_rows, width).astype(jnp.bfloat16)


def local(q_conv, k_conv, v_conv, conv_filter, q_attn, k_attn, v_attn, w_conv_out, w_attn_out):
    count_ctx = lax.axis_size(CTX)
    my_index = lax.axis_index(CTX)
    tok_rows = q_conv.shape[0]
    gated = (k_conv.astype(jnp.float32) * v_conv.astype(jnp.float32)).astype(jnp.bfloat16)
    conv = spectral_conv(gated, conv_filter, my_index, tok_rows, count_ctx)
    mixed = (q_conv.astype(jnp.float32) * conv.astype(jnp.float32)).astype(jnp.bfloat16)
    conv_part = jnp.dot(mixed, w_conv_out, preferred_element_type=jnp.float32)
    attended = attention(q_attn, k_attn, v_attn, tok_rows)
    return lax.psum_scatter(
        (conv_part + jnp.dot(attended, w_attn_out, preferred_element_type=jnp.float32)).astype(jnp.bfloat16),
        "ch",
        scatter_dimension=0,
        tiled=True,
    )


def solution(mesh):
    ctx_size, ch_size = mesh.devices.shape
    split_mesh = jax.sharding.Mesh(
        mesh.devices.reshape(ctx_size // 8, 2, 4, ch_size), CTX + ("ch",)
    )
    tokens = P(CTX, "ch")
    return jax.shard_map(
        local,
        mesh=split_mesh,
        in_specs=(tokens,) * 7 + (P("ch", None), P("ch", None)),
        out_specs=P(CTX + ("ch",), None),
        check_vma=False,
    )
```

```python
from functools import partial
import math

import jax
import jax.numpy as jnp
from jax import lax
from jax.sharding import PartitionSpec as P
from jax.experimental import pallas as pl
from jax.experimental.pallas import tpu as pltpu

HD = 128


two_pi = 2.0 * math.pi
neg_large = -1e30
highest = lax.Precision.HIGHEST


def angle_table(left_idx, right_idx, period):
    product = left_idx[:, None] * right_idx[None, :] % period
    return product.astype(jnp.float32) * (two_pi / period)


def section_coarse(values, cos_table, sin_table, twiddle):
    real_part = jnp.einsum("kn,nsc->ksc", cos_table, values, precision=highest)
    imag_part = -jnp.einsum("kn,nsc->ksc", sin_table, values, precision=highest)
    cos_twist = jnp.cos(twiddle)[:, :, None]
    sin_twist = jnp.sin(twiddle)[:, :, None]
    return (
        real_part * cos_twist + imag_part * sin_twist,
        imag_part * cos_twist - real_part * sin_twist,
    )


def section_fine(real_part, imag_part, cos_table, sin_table, direction):
    cos_real = jnp.einsum("kn,anc->akc", cos_table, real_part, precision=highest)
    cos_imag = jnp.einsum("kn,anc->akc", cos_table, imag_part, precision=highest)
    sin_real = jnp.einsum("kn,anc->akc", sin_table, real_part, precision=highest)
    sin_imag = jnp.einsum("kn,anc->akc", sin_table, imag_part, precision=highest)
    return (cos_real - direction * sin_imag, cos_imag + direction * sin_real)


def spectral_conv(gated, filters, my_index, tok_rows, count_ctx):
    chans = gated.shape[1]
    groups = filters.shape[1]
    share = chans // groups
    sub_rows = tok_rows // count_ctx
    period = 2 * count_ctx * tok_rows
    both = lax.all_to_all(
        jnp.concatenate([gated, filters], axis=1).reshape(1, tok_rows, chans + groups),
        CTX, split_axis=1, concat_axis=0, tiled=True,
    )
    got_source = both[:, :, :chans]
    got_filter = both[:, :, chans:]
    coarse_idx = jnp.arange(count_ctx, dtype=jnp.int32)
    coarse_freq = jnp.arange(2 * count_ctx, dtype=jnp.int32)
    coarse_angle = angle_table(coarse_freq, coarse_idx, 2 * count_ctx)
    cos_coarse = jnp.cos(coarse_angle)
    sin_coarse = jnp.sin(coarse_angle)
    fine_global = my_index * sub_rows + jnp.arange(sub_rows, dtype=jnp.int32)
    twist_in = angle_table(coarse_freq, fine_global, period)
    source_re, source_im = section_coarse(
        got_source.astype(jnp.float32), cos_coarse, sin_coarse, twist_in
    )
    filter_re, filter_im = section_coarse(
        got_filter.astype(jnp.float32), cos_coarse, sin_coarse, twist_in
    )
    packed = lax.all_to_all(
        jnp.concatenate([source_re, source_im, filter_re, filter_im], axis=2).astype(jnp.bfloat16),
        CTX, split_axis=0, concat_axis=1, tiled=True,
    ).astype(jnp.float32)
    source_re = packed[:, :, :chans]
    source_im = packed[:, :, chans:2 * chans]
    filter_re = packed[:, :, 2 * chans:2 * chans + groups]
    filter_im = packed[:, :, 2 * chans + groups:]
    fine_idx = jnp.arange(tok_rows, dtype=jnp.int32)
    fine_angle = angle_table(fine_idx, fine_idx, tok_rows)
    cos_fine = jnp.cos(fine_angle)
    sin_fine = jnp.sin(fine_angle)
    source_re, source_im = section_fine(source_re, source_im, cos_fine, sin_fine, -1.0)
    filter_re, filter_im = section_fine(filter_re, filter_im, cos_fine, sin_fine, -1.0)
    split_re = source_re.reshape(2, tok_rows, groups, share)
    split_im = source_im.reshape(2, tok_rows, groups, share)
    prod_re = split_re * filter_re[..., None] - split_im * filter_im[..., None]
    prod_im = split_re * filter_im[..., None] + split_im * filter_re[..., None]
    back_re, back_im = section_fine(
        prod_re.reshape(2, tok_rows, chans),
        prod_im.reshape(2, tok_rows, chans),
        cos_fine,
        sin_fine,
        1.0,
    )
    pair_freq = my_index * 2 + jnp.arange(2, dtype=jnp.int32)
    twist_out = angle_table(pair_freq, fine_idx, period)
    cos_out = jnp.cos(twist_out)[:, :, None]
    sin_out = jnp.sin(twist_out)[:, :, None]
    turned_re = back_re * cos_out - back_im * sin_out
    turned_im = back_re * sin_out + back_im * cos_out
    turned = lax.all_to_all(
        jnp.concatenate([turned_re, turned_im], axis=2).astype(jnp.bfloat16),
        CTX, split_axis=1, concat_axis=0, tiled=True,
    ).astype(jnp.float32)
    turned_re = turned[:, :, :chans]
    turned_im = turned[:, :, chans:]
    result = jnp.einsum("nk,ksc->nsc", cos_coarse.T, turned_re, precision=highest)
    result = result - jnp.einsum("nk,ksc->nsc", sin_coarse.T, turned_im, precision=highest)
    rounded = (result / period).astype(jnp.bfloat16)
    returned = lax.all_to_all(rounded, CTX, split_axis=0, concat_axis=1, tiled=True)
    return returned.reshape(tok_rows, chans)


CTX = ("z", "yh", "x")
EXP2_SCALE = math.log2(math.e) * HD ** (-0.5)
HALF = ("yh", "x")


def flash_kernel(info_ref, q_ref, k_ref, v_ref, acc_ref, m_ref, l_ref, *, heads, tok_rows, key_block, scale):
    j = pl.program_id(0)
    q_first = info_ref[0]
    last_block = info_ref[1] - 1
    key_first = j * key_block

    @pl.when(j == 0)
    def _():
        m_ref[...] = jnp.full_like(m_ref, neg_large)
        l_ref[...] = jnp.zeros_like(l_ref)
        acc_ref[...] = jnp.zeros_like(acc_ref)

    def step(masked):
        if masked:
            query_pos = q_first + lax.broadcasted_iota(jnp.int32, (tok_rows, key_block), 0)
            key_pos = key_first + lax.broadcasted_iota(jnp.int32, (tok_rows, key_block), 1)
            allowed = key_pos <= query_pos
        for h in range(heads):
            cols = slice(h * HD, (h + 1) * HD)
            scores = lax.dot_general(
                q_ref[:, cols], k_ref[:, cols], (((1,), (1,)), ((), ())),
                preferred_element_type=jnp.float32,
            )
            if masked:
                scores = jnp.where(allowed, scores, neg_large)
            m_prev = m_ref[h]
            m_new = jnp.maximum(m_prev, jnp.max(scores, axis=1, keepdims=True))
            weights = jnp.exp2((scores - m_new) * scale)
            if masked:
                weights = jnp.where(allowed, weights, 0.0)
            factor = jnp.exp2((m_prev - m_new) * scale)
            l_ref[h] = l_ref[h] * factor + jnp.sum(weights, axis=1, keepdims=True)
            acc_ref[:, cols] = acc_ref[:, cols] * factor + jnp.dot(
                weights.astype(jnp.bfloat16), v_ref[:, cols], preferred_element_type=jnp.float32
            )
            m_ref[h] = m_new

    full = key_first + key_block <= q_first

    @pl.when(jnp.logical_and(j <= last_block, full))
    def _():
        step(False)

    @pl.when(jnp.logical_and(j <= last_block, jnp.logical_not(full)))
    def _():
        step(True)


def flash_partial(queries, keys, values, q_first, needed, key_block):
    tok_rows, width = queries.shape
    heads = width // HD
    total_rows = keys.shape[0]
    info = jnp.stack([q_first, needed]).astype(jnp.int32)
    kernel = partial(flash_kernel, heads=heads, tok_rows=tok_rows, key_block=key_block, scale=EXP2_SCALE)
    kv_spec = pl.BlockSpec((key_block, width), lambda j, info: (jnp.minimum(j, info[1] - 1), 0))
    stat_spec = pl.BlockSpec((heads, tok_rows, 1), lambda j, info: (0, 0, 0))
    return pl.pallas_call(
        kernel,
        out_shape=(
            jax.ShapeDtypeStruct((tok_rows, width), jnp.float32),
            jax.ShapeDtypeStruct((heads, tok_rows, 1), jnp.float32),
            jax.ShapeDtypeStruct((heads, tok_rows, 1), jnp.float32),
        ),
        grid_spec=pltpu.PrefetchScalarGridSpec(
            num_scalar_prefetch=1,
            grid=(total_rows // key_block,),
            in_specs=[pl.BlockSpec((tok_rows, width), lambda j, info: (0, 0)), kv_spec, kv_spec],
            out_specs=[pl.BlockSpec((tok_rows, width), lambda j, info: (0, 0)), stat_spec, stat_spec],
        ),
        compiler_params=pltpu.CompilerParams(
            dimension_semantics=("arbitrary",), vmem_limit_bytes=48 * 1024 * 1024
        ),
        cost_estimate=pl.CostEstimate(
            flops=4 * tok_rows * total_rows * width,
            transcendentals=heads * tok_rows * total_rows,
            bytes_accessed=2 * total_rows * width * 2 + tok_rows * width * 6,
        ),
    )(info, queries, keys, values)


def attention(q_attn, k_attn, v_attn, tok_rows):
    width = q_attn.shape[1]
    heads = width // HD
    quarters = lax.axis_size("z")
    quarter = lax.axis_index("z")
    half_count = 1
    for name in HALF:
        half_count = half_count * lax.axis_size(name)
    my_index = lax.axis_index(CTX)
    local_index = my_index - quarter * half_count
    key_part = lax.all_gather(k_attn, HALF, axis=0, tiled=True)
    value_part = lax.all_gather(v_attn, HALF, axis=0, tiled=True)
    part_rows = key_part.shape[0]
    key_block = 896 if part_rows % 896 == 0 else tok_rows
    states = []
    shifts = list(range(1, quarters))
    visiting = jnp.concatenate(
        [lax.ppermute(q_attn, "z", [(k, k - shift) for k in range(shift, quarters)]) for shift in shifts]
    )
    needed = ((local_index + 1) * tok_rows + key_block - 1) // key_block
    own_acc, own_max, own_total = flash_partial(
        q_attn, key_part, value_part, local_index * tok_rows, needed, key_block
    )
    own_out, visiting = lax.optimization_barrier(((own_acc, own_max, own_total), visiting))
    own_acc, own_max, own_total = own_out
    cross = flash_partial(
        visiting, key_part, value_part, jnp.int32(part_rows), jnp.int32(part_rows // key_block), key_block
    )
    for slot, shift in enumerate(shifts):
        rows = slice(slot * tok_rows, (slot + 1) * tok_rows)
        stats = jnp.concatenate(
            [cross[1][:, rows].reshape(heads, tok_rows), cross[2][:, rows].reshape(heads, tok_rows)]
        )
        back = lax.ppermute(
            jnp.concatenate([cross[0][rows], stats.T], axis=1), "z", [(k - shift, k) for k in range(shift, quarters)]
        )
        back_stats = back[:, width:].T
        back_max = jnp.where(quarter >= shift, back_stats[:heads], neg_large)
        states.append((back[:, :width], back_max, back_stats[heads:]))
    states.append((own_acc, own_max.reshape(heads, tok_rows), own_total.reshape(heads, tok_rows)))
    top = states[0][1]
    for state in states[1:]:
        top = jnp.maximum(top, state[1])
    merged = None
    totals = None
    for acc, row_max, row_total in states:
        scale = jnp.exp2((row_max - top) * EXP2_SCALE)
        part = acc.reshape(tok_rows, heads, HD) * scale.T[:, :, None]
        merged = part if merged is None else merged + part
        totals = scale * row_total if totals is None else totals + scale * row_total
    merged = merged / totals.T[:, :, None]
    return merged.reshape(tok_rows, width).astype(jnp.bfloat16)


def local(q_conv, k_conv, v_conv, conv_filter, q_attn, k_attn, v_attn, w_conv_out, w_attn_out):
    count_ctx = lax.axis_size(CTX)
    my_index = lax.axis_index(CTX)
    tok_rows = q_conv.shape[0]
    gated = (k_conv.astype(jnp.float32) * v_conv.astype(jnp.float32)).astype(jnp.bfloat16)
    conv = spectral_conv(gated, conv_filter, my_index, tok_rows, count_ctx)
    mixed = (q_conv.astype(jnp.float32) * conv.astype(jnp.float32)).astype(jnp.bfloat16)
    conv_part = jnp.dot(mixed, w_conv_out, preferred_element_type=jnp.float32)
    attended = attention(q_attn, k_attn, v_attn, tok_rows)
    return lax.psum_scatter(
        (conv_part + jnp.dot(attended, w_attn_out, preferred_element_type=jnp.float32)).astype(jnp.bfloat16),
        "ch",
        scatter_dimension=0,
        tiled=True,
    )


def solution(mesh):
    ctx_size, ch_size = mesh.devices.shape
    split_mesh = jax.sharding.Mesh(
        mesh.devices.reshape(ctx_size // 8, 2, 4, ch_size), CTX + ("ch",)
    )
    tokens = P(CTX, "ch")
    return jax.shard_map(
        local,
        mesh=split_mesh,
        in_specs=(tokens,) * 7 + (P("ch", None), P("ch", None)),
        out_specs=P(CTX + ("ch",), None),
        check_vma=False,
    )
```

```python
from functools import partial
import math

import jax
import jax.numpy as jnp
from jax import lax
from jax.sharding import PartitionSpec as P
from jax.experimental import pallas as pl
from jax.experimental.pallas import tpu as pltpu

HD = 128


two_pi = 2.0 * math.pi
neg_large = -1e30
highest = lax.Precision.HIGHEST


def angle_table(left_idx, right_idx, period):
    product = left_idx[:, None] * right_idx[None, :] % period
    return product.astype(jnp.float32) * (two_pi / period)


def section_coarse(values, cos_table, sin_table, twiddle):
    real_part = jnp.einsum("kn,nsc->ksc", cos_table, values, precision=highest)
    imag_part = -jnp.einsum("kn,nsc->ksc", sin_table, values, precision=highest)
    cos_twist = jnp.cos(twiddle)[:, :, None]
    sin_twist = jnp.sin(twiddle)[:, :, None]
    return (
        real_part * cos_twist + imag_part * sin_twist,
        imag_part * cos_twist - real_part * sin_twist,
    )


def section_fine(real_part, imag_part, cos_table, sin_table, direction):
    cos_real = jnp.einsum("kn,anc->akc", cos_table, real_part, precision=highest)
    cos_imag = jnp.einsum("kn,anc->akc", cos_table, imag_part, precision=highest)
    sin_real = jnp.einsum("kn,anc->akc", sin_table, real_part, precision=highest)
    sin_imag = jnp.einsum("kn,anc->akc", sin_table, imag_part, precision=highest)
    return (cos_real - direction * sin_imag, cos_imag + direction * sin_real)


def spectral_conv(gated, filters, my_index, tok_rows, count_ctx):
    chans = gated.shape[1]
    groups = filters.shape[1]
    share = chans // groups
    sub_rows = tok_rows // count_ctx
    period = 2 * count_ctx * tok_rows
    both = lax.all_to_all(
        jnp.concatenate([gated, filters], axis=1).reshape(1, tok_rows, chans + groups),
        CTX, split_axis=1, concat_axis=0, tiled=True,
    )
    got_source = both[:, :, :chans]
    got_filter = both[:, :, chans:]
    coarse_idx = jnp.arange(count_ctx, dtype=jnp.int32)
    coarse_freq = jnp.arange(2 * count_ctx, dtype=jnp.int32)
    coarse_angle = angle_table(coarse_freq, coarse_idx, 2 * count_ctx)
    cos_coarse = jnp.cos(coarse_angle)
    sin_coarse = jnp.sin(coarse_angle)
    fine_global = my_index * sub_rows + jnp.arange(sub_rows, dtype=jnp.int32)
    twist_in = angle_table(coarse_freq, fine_global, period)
    source_re, source_im = section_coarse(
        got_source.astype(jnp.float32), cos_coarse, sin_coarse, twist_in
    )
    filter_re, filter_im = section_coarse(
        got_filter.astype(jnp.float32), cos_coarse, sin_coarse, twist_in
    )
    packed = lax.all_to_all(
        jnp.concatenate([source_re, source_im, filter_re, filter_im], axis=2).astype(jnp.bfloat16),
        CTX, split_axis=0, concat_axis=1, tiled=True,
    ).astype(jnp.float32)
    source_re = packed[:, :, :chans]
    source_im = packed[:, :, chans:2 * chans]
    filter_re = packed[:, :, 2 * chans:2 * chans + groups]
    filter_im = packed[:, :, 2 * chans + groups:]
    fine_idx = jnp.arange(tok_rows, dtype=jnp.int32)
    fine_angle = angle_table(fine_idx, fine_idx, tok_rows)
    cos_fine = jnp.cos(fine_angle)
    sin_fine = jnp.sin(fine_angle)
    source_re, source_im = section_fine(source_re, source_im, cos_fine, sin_fine, -1.0)
    filter_re, filter_im = section_fine(filter_re, filter_im, cos_fine, sin_fine, -1.0)
    split_re = source_re.reshape(2, tok_rows, groups, share)
    split_im = source_im.reshape(2, tok_rows, groups, share)
    prod_re = split_re * filter_re[..., None] - split_im * filter_im[..., None]
    prod_im = split_re * filter_im[..., None] + split_im * filter_re[..., None]
    back_re, back_im = section_fine(
        prod_re.reshape(2, tok_rows, chans),
        prod_im.reshape(2, tok_rows, chans),
        cos_fine,
        sin_fine,
        1.0,
    )
    pair_freq = my_index * 2 + jnp.arange(2, dtype=jnp.int32)
    twist_out = angle_table(pair_freq, fine_idx, period)
    cos_out = jnp.cos(twist_out)[:, :, None]
    sin_out = jnp.sin(twist_out)[:, :, None]
    turned_re = back_re * cos_out - back_im * sin_out
    turned_im = back_re * sin_out + back_im * cos_out
    turned = lax.all_to_all(
        jnp.concatenate([turned_re, turned_im], axis=2).astype(jnp.bfloat16),
        CTX, split_axis=1, concat_axis=0, tiled=True,
    ).astype(jnp.float32)
    turned_re = turned[:, :, :chans]
    turned_im = turned[:, :, chans:]
    result = jnp.einsum("nk,ksc->nsc", cos_coarse.T, turned_re, precision=highest)
    result = result - jnp.einsum("nk,ksc->nsc", sin_coarse.T, turned_im, precision=highest)
    rounded = (result / period).astype(jnp.bfloat16)
    returned = lax.all_to_all(rounded, CTX, split_axis=0, concat_axis=1, tiled=True)
    return returned.reshape(tok_rows, chans)


CTX = ("z", "yh", "x")
EXP2_SCALE = math.log2(math.e) * HD ** (-0.5)
HALF = ("yh", "x")


def flash_kernel(info_ref, q_ref, k_ref, v_ref, acc_ref, m_ref, l_ref, *, heads, tok_rows, key_block, scale):
    j = pl.program_id(0)
    q_first = info_ref[0]
    last_block = info_ref[1] - 1
    key_first = j * key_block

    @pl.when(j == 0)
    def _():
        m_ref[...] = jnp.full_like(m_ref, neg_large)
        l_ref[...] = jnp.zeros_like(l_ref)
        acc_ref[...] = jnp.zeros_like(acc_ref)

    def step(masked):
        if masked:
            query_pos = q_first + lax.broadcasted_iota(jnp.int32, (tok_rows, key_block), 0)
            key_pos = key_first + lax.broadcasted_iota(jnp.int32, (tok_rows, key_block), 1)
            allowed = key_pos <= query_pos
        for h in range(heads):
            cols = slice(h * HD, (h + 1) * HD)
            scores = lax.dot_general(
                q_ref[:, cols], k_ref[:, cols], (((1,), (1,)), ((), ())),
                preferred_element_type=jnp.float32,
            )
            if masked:
                scores = jnp.where(allowed, scores, neg_large)
            m_prev = m_ref[h]
            m_new = jnp.maximum(m_prev, jnp.max(scores, axis=1, keepdims=True))
            weights = jnp.exp2((scores - m_new) * scale)
            if masked:
                weights = jnp.where(allowed, weights, 0.0)
            factor = jnp.exp2((m_prev - m_new) * scale)
            l_ref[h] = l_ref[h] * factor + jnp.sum(weights, axis=1, keepdims=True)
            acc_ref[:, cols] = acc_ref[:, cols] * factor + jnp.dot(
                weights.astype(jnp.bfloat16), v_ref[:, cols], preferred_element_type=jnp.float32
            )
            m_ref[h] = m_new

    full = key_first + key_block <= q_first

    @pl.when(jnp.logical_and(j <= last_block, full))
    def _():
        step(False)

    @pl.when(jnp.logical_and(j <= last_block, jnp.logical_not(full)))
    def _():
        step(True)


def flash_partial(queries, keys, values, q_first, needed, key_block):
    tok_rows, width = queries.shape
    heads = width // HD
    total_rows = keys.shape[0]
    info = jnp.stack([q_first, needed]).astype(jnp.int32)
    kernel = partial(flash_kernel, heads=heads, tok_rows=tok_rows, key_block=key_block, scale=EXP2_SCALE)
    kv_spec = pl.BlockSpec((key_block, width), lambda j, info: (jnp.minimum(j, info[1] - 1), 0))
    stat_spec = pl.BlockSpec((heads, tok_rows, 1), lambda j, info: (0, 0, 0))
    return pl.pallas_call(
        kernel,
        out_shape=(
            jax.ShapeDtypeStruct((tok_rows, width), jnp.float32),
            jax.ShapeDtypeStruct((heads, tok_rows, 1), jnp.float32),
            jax.ShapeDtypeStruct((heads, tok_rows, 1), jnp.float32),
        ),
        grid_spec=pltpu.PrefetchScalarGridSpec(
            num_scalar_prefetch=1,
            grid=(total_rows // key_block,),
            in_specs=[pl.BlockSpec((tok_rows, width), lambda j, info: (0, 0)), kv_spec, kv_spec],
            out_specs=[pl.BlockSpec((tok_rows, width), lambda j, info: (0, 0)), stat_spec, stat_spec],
        ),
        compiler_params=pltpu.CompilerParams(
            dimension_semantics=("arbitrary",), vmem_limit_bytes=48 * 1024 * 1024
        ),
        cost_estimate=pl.CostEstimate(
            flops=4 * tok_rows * total_rows * width,
            transcendentals=heads * tok_rows * total_rows,
            bytes_accessed=2 * total_rows * width * 2 + tok_rows * width * 6,
        ),
    )(info, queries, keys, values)


def attention(q_attn, k_attn, v_attn, tok_rows):
    width = q_attn.shape[1]
    heads = width // HD
    quarters = lax.axis_size("z")
    quarter = lax.axis_index("z")
    half_count = 1
    for name in HALF:
        half_count = half_count * lax.axis_size(name)
    my_index = lax.axis_index(CTX)
    local_index = my_index - quarter * half_count
    key_part = lax.all_gather(k_attn, HALF, axis=0, tiled=True)
    value_part = lax.all_gather(v_attn, HALF, axis=0, tiled=True)
    part_rows = key_part.shape[0]
    key_block = 896 if part_rows % 896 == 0 else tok_rows
    states = []
    for shift in range(1, quarters):
        visiting = lax.ppermute(q_attn, "z", [(k, k - shift) for k in range(shift, quarters)])
        cross = flash_partial(
            visiting, key_part, value_part, jnp.int32(part_rows), jnp.int32(part_rows // key_block), key_block
        )
        stats = jnp.concatenate([cross[1].reshape(heads, tok_rows), cross[2].reshape(heads, tok_rows)])
        back_acc, back_stats = lax.ppermute(
            (cross[0], stats), "z", [(k - shift, k) for k in range(shift, quarters)]
        )
        back_max = jnp.where(quarter >= shift, back_stats[:heads], neg_large)
        states.append((back_acc, back_max, back_stats[heads:]))
    needed = ((local_index + 1) * tok_rows + key_block - 1) // key_block
    own_acc, own_max, own_total = flash_partial(
        q_attn, key_part, value_part, local_index * tok_rows, needed, key_block
    )
    states.append((own_acc, own_max.reshape(heads, tok_rows), own_total.reshape(heads, tok_rows)))
    top = states[0][1]
    for state in states[1:]:
        top = jnp.maximum(top, state[1])
    merged = None
    totals = None
    for acc, row_max, row_total in states:
        scale = jnp.exp2((row_max - top) * EXP2_SCALE)
        part = acc.reshape(tok_rows, heads, HD) * scale.T[:, :, None]
        merged = part if merged is None else merged + part
        totals = scale * row_total if totals is None else totals + scale * row_total
    merged = merged / totals.T[:, :, None]
    return merged.reshape(tok_rows, width).astype(jnp.bfloat16)


def local(q_conv, k_conv, v_conv, conv_filter, q_attn, k_attn, v_attn, w_conv_out, w_attn_out):
    count_ctx = lax.axis_size(CTX)
    my_index = lax.axis_index(CTX)
    tok_rows = q_conv.shape[0]
    gated = (k_conv.astype(jnp.float32) * v_conv.astype(jnp.float32)).astype(jnp.bfloat16)
    conv = spectral_conv(gated, conv_filter, my_index, tok_rows, count_ctx)
    mixed = (q_conv.astype(jnp.float32) * conv.astype(jnp.float32)).astype(jnp.bfloat16)
    attended = attention(q_attn, k_attn, v_attn, tok_rows)
    half = w_conv_out.shape[1] // 2
    outs = []
    for cols in (slice(0, half), slice(half, 2 * half)):
        part = (
            jnp.dot(mixed, w_conv_out[:, cols], preferred_element_type=jnp.float32)
            + jnp.dot(attended, w_attn_out[:, cols], preferred_element_type=jnp.float32)
        ).astype(jnp.bfloat16)
        outs.append(lax.psum_scatter(part, "ch", scatter_dimension=0, tiled=True))
    return jnp.concatenate(outs, axis=1)


def solution(mesh):
    ctx_size, ch_size = mesh.devices.shape
    split_mesh = jax.sharding.Mesh(
        mesh.devices.reshape(ctx_size // 8, 2, 4, ch_size), CTX + ("ch",)
    )
    tokens = P(CTX, "ch")
    return jax.shard_map(
        local,
        mesh=split_mesh,
        in_specs=(tokens,) * 7 + (P("ch", None), P("ch", None)),
        out_specs=P(CTX + ("ch",), None),
        check_vma=False,
    )
```
